32 devices in a mesh: section: 2 (over x), fsdp: 4 (over z), dp: 4 (over y, core).
Axes of the slice: x: 2, y: 2, z: 4, core: 2. Of those that a mesh axis runs over, the one named last changes fastest.
Arguments:
- activations: bfloat16 [2, 4, 512, 3584], P('section', None, ('fsdp', 'dp')), may hold values from -6 to 6
- out_grad: bfloat16 [2, 4, 512, 14336], P('section', None, ('fsdp', 'dp')), may hold values from -6 to 6
- blocks: bfloat16 [2, 16, 128, 128], P('section', 'fsdp'), may hold values from -0.5 to 0.5
- pattern: int32 [2, 16, 2], P('section', 'fsdp'), may hold values from 0 to 111, as said below
- order: int32 [4], replicated, may hold values from 0 to 3, each once
Outputs:
- received: bfloat16 [2, 4, 512, 3584], P('section', None, ('fsdp', 'dp'))
- weight_grad: float32 [2, 16, 128, 128], P('section', 'fsdp')
The draws below stay inside these ranges and needn't reach their ends.
Inputs may be any that keep to these rules, and one draw needn't show every extreme that they name: pattern[s, b, 0] < 28 and pattern[s, b, 1] < 112; no two blocks of one section share both indices; within a section the blocks stand in ascending order of (row, column). `order`: a permutation of the microbatches.
All inputs are finite; a program needn't handle non-finite values.
Results may differ from the reference program's by a relative error of at most 0.0049.
Values may be sent and summed in bfloat16 or wider, within the bound.
No kernel may reach another device: no remote copies, remote signals or barrier semaphores. Data moves between devices by JAX's collectives and lax.ppermute only.
A program may use at most 128 MiB of HBM per device.

```python
import jax
import jax.numpy as jnp
from jax import lax

D = 3584
FF = 14336
BLOCK = 128
ROW_BLOCKS = 28
COL_BLOCKS = 112
NB_DEV = 4
NB = 16
MICRO = 4
TOK_MB = 32
ROWS = 512
N_SECTION = 2
N_FSDP = 4
N_DP = 4


def draw_pattern(key, part):
    cells_all = ROW_BLOCKS * COL_BLOCKS

    def one_section(section_key):
        middle = jax.random.permutation(section_key, cells_all - 2)[:NB_DEV * N_FSDP - 2] + 1
        chosen = jnp.concatenate([jnp.zeros((1,), jnp.int32), middle.astype(jnp.int32), jnp.full((1,), cells_all - 1, jnp.int32)])
        chosen = jnp.sort(chosen)
        return jnp.stack([chosen // COL_BLOCKS, chosen % COL_BLOCKS], axis=1).astype(jnp.int32)
    section_keys = jax.random.split(jax.random.fold_in(key, 7), N_SECTION)
    return jax.vmap(one_section)(section_keys)


def levels(key, extent, shards, low, largest):
    loudness = 1.0
    for axis_at, shards_of in shards:
        draws = jax.random.uniform(jax.random.fold_in(jax.random.fold_in(key, 6), axis_at), (shards_of,), jnp.float32, low / len(shards), largest / len(shards))
        loudness = loudness * jnp.repeat(jnp.exp(draws), extent[axis_at] // shards_of).reshape((-1,) + (1,) * (len(extent) - 1 - axis_at))
    return loudness


def gaussian(key, extent, spread, bound, pieces=(), kind=jnp.bfloat16):
    values = spread * jax.random.normal(key, extent, jnp.float32)
    if pieces:
        values = values * levels(key, extent, pieces, -0.22, 0.18)
    return jnp.clip(values, -bound, bound).astype(kind)


def setup_inputs(seed: int = 0) -> dict:
    seeds = jax.random.split(jax.random.key(seed), 6)
    return {
        "activations": gaussian(seeds[0], (N_SECTION, MICRO, ROWS, D), 1.0, 6.0, ((0, 2), (2, 16))),
        "out_grad": gaussian(seeds[1], (N_SECTION, MICRO, ROWS, FF), 1.0, 6.0, ((0, 2), (2, 16))),
        "blocks": gaussian(seeds[2], (N_SECTION, NB, BLOCK, BLOCK), (BLOCK * max(1, NB // COL_BLOCKS)) ** -0.5, 0.5, ((0, 2), (1, 4))),
        "pattern": draw_pattern(jax.random.fold_in(seeds[5], 71), 0),
        "order": jax.random.permutation(seeds[4], MICRO).astype(jnp.int32),
    }


def silu_slope(pre_act):
    sigmoid_val = jax.nn.sigmoid(pre_act)
    return sigmoid_val * (1.0 + pre_act * (1.0 - sigmoid_val))

def device_pass(features, hidden_grad, weights, row_ids, col_ids):
    tokens_dev = features.shape[0]
    rows_in = jnp.take(features, row_ids, axis=1).astype(jnp.float32)
    product = jnp.einsum('tbk,bkn->tbn', rows_in, weights)
    pre_act = jnp.zeros((tokens_dev, COL_BLOCKS, BLOCK), jnp.float32).at[:, col_ids].add(product)
    act_grad = (hidden_grad.astype(jnp.float32) * silu_slope(pre_act.reshape(tokens_dev, FF))).astype(jnp.bfloat16)
    grad_cols = act_grad.reshape(tokens_dev, COL_BLOCKS, BLOCK)
    cols_in = jnp.take(grad_cols, col_ids, axis=1).astype(jnp.float32)
    backward = jnp.einsum('tbn,bkn->tbk', cols_in, weights)
    input_grad = jnp.zeros((tokens_dev, ROW_BLOCKS, BLOCK), jnp.float32).at[:, row_ids].add(backward)
    input_grad = input_grad.astype(jnp.bfloat16).reshape(tokens_dev, D)
    partial_grad = jnp.einsum('tbk,tbn->bkn', rows_in, cols_in)
    return (input_grad, partial_grad)

def reference(activations, out_grad, blocks, pattern, order):
    groups = N_FSDP * N_DP
    grad_list = []
    inputs_list = []
    for section_idx in range(N_SECTION):
        features = activations[section_idx].reshape(MICRO, groups, TOK_MB, ROW_BLOCKS, BLOCK)
        features = features.transpose(1, 0, 2, 3, 4).reshape(groups, MICRO * TOK_MB, ROW_BLOCKS, BLOCK)
        hidden = out_grad[section_idx].reshape(MICRO, groups, TOK_MB, FF)
        hidden = hidden.transpose(1, 0, 2, 3).reshape(groups, MICRO * TOK_MB, FF)
        row_ids = pattern[section_idx, :, 0].astype(jnp.int32)
        col_ids = pattern[section_idx, :, 1].astype(jnp.int32)
        weights = blocks[section_idx].astype(jnp.float32)

        def one_group(running, group_data):
            input_grad, partial_grad = device_pass(group_data[0], group_data[1], weights, row_ids, col_ids)
            return (running + partial_grad, input_grad)
        running, grads_in = lax.scan(one_group, jnp.zeros((NB, BLOCK, BLOCK), jnp.float32), (features, hidden))
        grad_list.append(running / jnp.sqrt(jnp.float32(MICRO * ROWS)))
        grad_rows = grads_in.reshape(groups, MICRO, TOK_MB, D).transpose(1, 0, 2, 3).reshape(MICRO, ROWS, D)
        inputs_list.append(jnp.take(grad_rows, order, axis=0))
    received = jnp.stack(inputs_list[1:] + [jnp.zeros_like(inputs_list[0])])
    return (received, jnp.stack(grad_list))
```

```python
import math

import jax
import jax.numpy as jnp
from jax import lax
from jax.sharding import PartitionSpec as P


def passed_along(block, axis, distance):
    devices = range(lax.axis_size(axis))
    route = [(i - distance, i) for i in devices if i - distance in devices]
    return lax.ppermute(block, axis, route)


def shifted(x, axis, k):
    n = lax.axis_size(axis)
    return lax.ppermute(x, axis, [(i, (i + k) % n) for i in range(n)])


def swapped(x, axis, bit):
    n = lax.axis_size(axis)
    return lax.ppermute(x, axis, [(i, i ^ (1 << bit)) for i in range(n)])


def silu_slope(pre_act):
    sigmoid_val = jax.nn.sigmoid(pre_act)
    return sigmoid_val * (1.0 + pre_act * (1.0 - sigmoid_val))


def gather_over(x, axis):
    n = lax.axis_size(axis)
    return jnp.stack([x] + [shifted(x, axis, k) for k in range(1, n)])


def butterfly_gather(x, axis, bits):
    me = lax.axis_index(axis)
    held = x
    for bit in bits:
        other = swapped(held, axis, bit)
        mine_low = ((me >> bit) & 1) == 0
        held = jnp.where(mine_low, jnp.stack([held, other]), jnp.stack([other, held]))
    order = sorted(range(len(bits)), key=lambda a: -bits[len(bits) - 1 - a])
    perm = [order[i] for i in range(len(bits))] + list(range(len(bits), held.ndim))
    return jnp.transpose(held, perm)


def local(activations, out_grad, blocks, pattern, order):
    block_size = blocks.shape[-1]
    micro_count = activations.shape[1]
    tok_rows = activations.shape[1] * activations.shape[2]
    row_count = activations.shape[3] // block_size
    col_count = out_grad.shape[3] // block_size
    n_fsdp = lax.axis_size("fsdp")
    n_dp = lax.axis_size("dp")
    dp_bits = int(round(math.log2(n_dp)))
    assert 1 << dp_bits == n_dp and block_size % n_dp == 0
    chunk = block_size // n_dp
    me_dp = lax.axis_index("dp")

    features = activations[0].reshape(tok_rows, row_count, block_size)
    hidden_grad = out_grad[0].reshape(tok_rows, col_count, block_size)
    own_blocks = blocks[0]
    blocks_dev = own_blocks.shape[0]

    all_indices = gather_over(pattern[0], "fsdp").reshape(-1, 2)

    own_chunk = lax.dynamic_slice_in_dim(own_blocks, me_dp * chunk, chunk, 1)
    fetched = gather_over(own_chunk, "fsdp")
    gathered = butterfly_gather(fetched, "dp", list(reversed(range(dp_bits))))
    gathered = gathered.reshape((n_dp, n_fsdp, blocks_dev, chunk, block_size))
    weights = jnp.transpose(gathered, (1, 2, 0, 3, 4)).reshape(
        n_fsdp * blocks_dev, block_size, block_size
    )

    row_ids = all_indices[:, 0]
    col_ids = all_indices[:, 1]
    rows_in = jnp.take(features, row_ids, axis=1)
    product = jnp.einsum(
        "tbk,bkn->tbn", rows_in, weights, preferred_element_type=jnp.float32
    )
    same_col = (col_ids[:, None] == col_ids[None, :]).astype(jnp.float32)
    pre_act = jnp.einsum(
        "bc,tcn->tbn", same_col, product, precision=lax.Precision.HIGHEST
    )
    hidden_in = jnp.take(hidden_grad, col_ids, axis=1)
    act_cols = (hidden_in.astype(jnp.float32) * silu_slope(pre_act)).astype(jnp.bfloat16)

    backward = jnp.einsum(
        "tbn,bkn->tbk", act_cols, weights, preferred_element_type=jnp.float32
    )
    row_hit = (jnp.arange(row_count, dtype=jnp.int32)[:, None] == row_ids[None, :]).astype(
        jnp.float32
    )
    input_grad = jnp.einsum(
        "rb,tbk->trk", row_hit, backward, precision=lax.Precision.HIGHEST
    )
    input_grad = input_grad.astype(jnp.bfloat16).reshape(
        micro_count, activations.shape[2], activations.shape[3]
    )
    ordered = jnp.take(input_grad, order, axis=0)
    received = passed_along(ordered, "section", -1)

    partial = jnp.einsum(
        "tbk,tbn->bkn", rows_in, act_cols, preferred_element_type=jnp.float32
    )
    held = partial.reshape((n_fsdp, blocks_dev) + (2,) * dp_bits + (chunk, block_size))
    for bit in range(dp_bits):
        axis_at = 2 + (dp_bits - 1 - bit)
        mine = (me_dp >> bit) & 1
        keep = lax.dynamic_index_in_dim(held, mine, axis_at, keepdims=False)
        send = lax.dynamic_index_in_dim(held, 1 - mine, axis_at, keepdims=False)
        held = keep + swapped(send, "dp", bit)
    owned = held[0]
    for k in range(1, n_fsdp):
        owned = owned + shifted(held[k], "fsdp", -k)
    full = butterfly_gather(owned, "dp", list(reversed(range(dp_bits))))
    full = full.reshape((n_dp, blocks_dev, chunk, block_size))
    full = jnp.transpose(full, (1, 0, 2, 3)).reshape(blocks_dev, block_size, block_size)
    grad_scale = jnp.sqrt(jnp.float32(tok_rows * n_fsdp * n_dp))
    return (received[None], (full / grad_scale)[None])


def solution(mesh):
    in_specs = (
        P("section", None, ("fsdp", "dp"), None),
        P("section", None, ("fsdp", "dp"), None),
        P("section", "fsdp", None, None),
        P("section", "fsdp", None),
        P(),
    )
    out_specs = (P("section", None, ("fsdp", "dp"), None), P("section", "fsdp", None, None))
    return jax.shard_map(local, mesh=mesh, in_specs=in_specs, out_specs=out_specs, check_vma=False)
```

```python
import math

import jax
import jax.numpy as jnp
from jax import lax
from jax.sharding import PartitionSpec as P


def passed_along(block, axis, distance):
    devices = range(lax.axis_size(axis))
    route = [(i - distance, i) for i in devices if i - distance in devices]
    return lax.ppermute(block, axis, route)


def shifted(x, axis, k):
    n = lax.axis_size(axis)
    return lax.ppermute(x, axis, [(i, (i + k) % n) for i in range(n)])


def swapped(x, axis, bit):
    n = lax.axis_size(axis)
    return lax.ppermute(x, axis, [(i, i ^ (1 << bit)) for i in range(n)])


def silu_slope(pre_act):
    sigmoid_val = jax.nn.sigmoid(pre_act)
    return sigmoid_val * (1.0 + pre_act * (1.0 - sigmoid_val))


def gather_over(x, axis):
    n = lax.axis_size(axis)
    return jnp.stack([x] + [shifted(x, axis, k) for k in range(1, n)])


def butterfly_gather(x, axis, bits):
    me = lax.axis_index(axis)
    held = x
    for bit in bits:
        other = swapped(held, axis, bit)
        mine_low = ((me >> bit) & 1) == 0
        held = jnp.where(mine_low, jnp.stack([held, other]), jnp.stack([other, held]))
    order = sorted(range(len(bits)), key=lambda a: -bits[len(bits) - 1 - a])
    perm = [order[i] for i in range(len(bits))] + list(range(len(bits), held.ndim))
    return jnp.transpose(held, perm)


def local(activations, out_grad, blocks, pattern, order):
    block_size = blocks.shape[-1]
    micro_count = activations.shape[1]
    tok_rows = activations.shape[1] * activations.shape[2]
    row_count = activations.shape[3] // block_size
    col_count = out_grad.shape[3] // block_size
    n_fsdp = lax.axis_size("fsdp")
    n_dp = lax.axis_size("dp")
    dp_bits = int(round(math.log2(n_dp)))
    assert 1 << dp_bits == n_dp and block_size % n_dp == 0
    chunk = block_size // n_dp
    me_dp = lax.axis_index("dp")

    own_blocks = blocks[0]
    blocks_dev = own_blocks.shape[0]

    assert n_fsdp % n_dp == 0
    per_dp = n_fsdp // n_dp
    weight_len = blocks_dev * block_size * block_size
    payload = jnp.concatenate(
        [own_blocks.reshape(-1), pattern[0].reshape(-1).astype(jnp.bfloat16)]
    )
    fetched = []
    for m in range(per_dp):
        pairs = []
        for f in range(n_fsdp):
            for d in range(n_dp):
                k = d + n_dp * m
                pairs.append((((f - k) % n_fsdp) * n_dp + d, f * n_dp + d))
        fetched.append(lax.ppermute(payload, ("fsdp", "dp"), pairs))
    fetched = jnp.stack(fetched)
    pieces = butterfly_gather(fetched, "dp", list(reversed(range(dp_bits))))
    pieces = pieces.reshape((n_dp, per_dp, -1))
    pieces = jnp.transpose(pieces, (1, 0, 2)).reshape(n_fsdp, -1)
    weights = pieces[:, :weight_len].reshape(n_fsdp * blocks_dev, block_size, block_size)
    all_indices = pieces[:, weight_len:].reshape(n_fsdp * blocks_dev, 2).astype(jnp.int32)
    block_count = n_fsdp * blocks_dev

    row_ids = all_indices[:, 0]
    col_ids = all_indices[:, 1]
    features = activations[0].reshape(tok_rows, -1)
    hidden_grad = out_grad[0].reshape(tok_rows, -1)
    rows_in = jnp.stack(
        [
            lax.dynamic_slice(features, (0, row_ids[b] * block_size), (tok_rows, block_size))
            for b in range(block_count)
        ]
    )
    hidden_in = jnp.stack(
        [
            lax.dynamic_slice(hidden_grad, (0, col_ids[b] * block_size), (tok_rows, block_size))
            for b in range(block_count)
        ]
    )
    tok_mb = activations.shape[2]
    rows_in = jnp.take(
        rows_in.reshape(block_count, micro_count, tok_mb, block_size), order, axis=1
    ).reshape(block_count, tok_rows, block_size)
    hidden_in = jnp.take(
        hidden_in.reshape(block_count, micro_count, tok_mb, block_size), order, axis=1
    ).reshape(block_count, tok_rows, block_size)

    product = jnp.einsum(
        "btk,bkn->btn", rows_in, weights, preferred_element_type=jnp.float32
    )
    same_col = (col_ids[:, None] == col_ids[None, :]).astype(jnp.float32)
    pre_act = jnp.einsum(
        "bc,ctn->btn", same_col, product, precision=lax.Precision.HIGHEST
    )
    act_cols = (hidden_in.astype(jnp.float32) * silu_slope(pre_act)).astype(jnp.bfloat16)

    backward = jnp.einsum(
        "btn,bkn->btk", act_cols, weights, preferred_element_type=jnp.float32
    )
    row_hit = (jnp.arange(row_count, dtype=jnp.int32)[:, None] == row_ids[None, :]).astype(
        jnp.float32
    )
    input_grad = jnp.einsum(
        "rb,btk->trk", row_hit, backward, precision=lax.Precision.HIGHEST
    )
    ordered = input_grad.astype(jnp.bfloat16).reshape(
        micro_count, tok_mb, activations.shape[3]
    )
    received = passed_along(ordered, "section", -1)

    partial = jnp.einsum(
        "btk,btn->bkn", rows_in, act_cols, preferred_element_type=jnp.float32
    )
    held = partial.reshape((n_fsdp, blocks_dev) + (2,) * dp_bits + (chunk, block_size))
    for bit in range(dp_bits):
        axis_at = 2 + (dp_bits - 1 - bit)
        mine = (me_dp >> bit) & 1
        keep = lax.dynamic_index_in_dim(held, mine, axis_at, keepdims=False)
        send = lax.dynamic_index_in_dim(held, 1 - mine, axis_at, keepdims=False)
        held = keep + swapped(send, "dp", bit)
    owned = held[0]
    for k in range(1, n_fsdp):
        owned = owned + shifted(held[k], "fsdp", -k)
    full = butterfly_gather(owned, "dp", list(reversed(range(dp_bits))))
    full = full.reshape((n_dp, blocks_dev, chunk, block_size))
    full = jnp.transpose(full, (1, 0, 2, 3)).reshape(blocks_dev, block_size, block_size)
    grad_scale = jnp.sqrt(jnp.float32(tok_rows * n_fsdp * n_dp))
    return (received[None], (full / grad_scale)[None])


def solution(mesh):
    in_specs = (
        P("section", None, ("fsdp", "dp"), None),
        P("section", None, ("fsdp", "dp"), None),
        P("section", "fsdp", None, None),
        P("section", "fsdp", None),
        P(),
    )
    out_specs = (P("section", None, ("fsdp", "dp"), None), P("section", "fsdp", None, None))
    return jax.shard_map(local, mesh=mesh, in_specs=in_specs, out_specs=out_specs, check_vma=False)
```

```python
import math

import jax
import jax.numpy as jnp
from jax import lax
from jax.sharding import PartitionSpec as P


def passed_along(block, axis, distance):
    devices = range(lax.axis_size(axis))
    route = [(i - distance, i) for i in devices if i - distance in devices]
    return lax.ppermute(block, axis, route)


def shifted(x, axis, k):
    n = lax.axis_size(axis)
    return lax.ppermute(x, axis, [(i, (i + k) % n) for i in range(n)])


def swapped(x, axis, bit):
    n = lax.axis_size(axis)
    return lax.ppermute(x, axis, [(i, i ^ (1 << bit)) for i in range(n)])


def silu_slope(pre_act):
    sigmoid_val = jax.nn.sigmoid(pre_act)
    return sigmoid_val * (1.0 + pre_act * (1.0 - sigmoid_val))


def gather_over(x, axis):
    n = lax.axis_size(axis)
    return jnp.stack([x] + [shifted(x, axis, k) for k in range(1, n)])


def butterfly_gather(x, axis, bits):
    me = lax.axis_index(axis)
    held = x
    for bit in bits:
        other = swapped(held, axis, bit)
        mine_low = ((me >> bit) & 1) == 0
        held = jnp.where(mine_low, jnp.stack([held, other]), jnp.stack([other, held]))
    order = sorted(range(len(bits)), key=lambda a: -bits[len(bits) - 1 - a])
    perm = [order[i] for i in range(len(bits))] + list(range(len(bits), held.ndim))
    return jnp.transpose(held, perm)


def local(activations, out_grad, blocks, pattern, order):
    block_size = blocks.shape[-1]
    micro_count = activations.shape[1]
    tok_rows = activations.shape[1] * activations.shape[2]
    row_count = activations.shape[3] // block_size
    col_count = out_grad.shape[3] // block_size
    n_fsdp = lax.axis_size("fsdp")
    n_dp = lax.axis_size("dp")
    dp_bits = int(round(math.log2(n_dp)))
    assert 1 << dp_bits == n_dp and block_size % n_dp == 0
    chunk = block_size // n_dp
    me_dp = lax.axis_index("dp")

    own_blocks = blocks[0]
    blocks_dev = own_blocks.shape[0]

    assert n_fsdp % n_dp == 0
    per_dp = n_fsdp // n_dp
    weight_len = blocks_dev * block_size * block_size
    payload = jnp.concatenate(
        [own_blocks.reshape(-1), pattern[0].reshape(-1).astype(jnp.bfloat16)]
    )
    fetched = []
    for m in range(per_dp):
        pairs = []
        for f in range(n_fsdp):
            for d in range(n_dp):
                k = d + n_dp * m
                pairs.append((((f - k) % n_fsdp) * n_dp + d, f * n_dp + d))
        fetched.append(lax.ppermute(payload, ("fsdp", "dp"), pairs))
    fetched = jnp.stack(fetched)
    pieces = butterfly_gather(fetched, "dp", list(reversed(range(dp_bits))))
    pieces = pieces.reshape((n_dp, per_dp, -1))
    pieces = jnp.transpose(pieces, (1, 0, 2)).reshape(n_fsdp, -1)
    weights = pieces[:, :weight_len].reshape(n_fsdp * blocks_dev, block_size, block_size)
    all_indices = pieces[:, weight_len:].reshape(n_fsdp * blocks_dev, 2).astype(jnp.int32)

    features = activations[0].reshape(tok_rows, row_count, block_size)
    hidden_grad = out_grad[0].reshape(tok_rows, col_count, block_size)
    row_ids = all_indices[:, 0]
    col_ids = all_indices[:, 1]
    rows_in = jnp.take(features, row_ids, axis=1)
    product = jnp.einsum(
        "tbk,bkn->tbn", rows_in, weights, preferred_element_type=jnp.float32
    )
    same_col = (col_ids[:, None] == col_ids[None, :]).astype(jnp.float32)
    pre_act = jnp.einsum(
        "bc,tcn->tbn", same_col, product, precision=lax.Precision.HIGHEST
    )
    hidden_in = jnp.take(hidden_grad, col_ids, axis=1)
    act_cols = (hidden_in.astype(jnp.float32) * silu_slope(pre_act)).astype(jnp.bfloat16)

    backward = jnp.einsum(
        "tbn,bkn->tbk", act_cols, weights, preferred_element_type=jnp.float32
    )
    row_hit = (jnp.arange(row_count, dtype=jnp.int32)[:, None] == row_ids[None, :]).astype(
        jnp.float32
    )
    input_grad = jnp.einsum(
        "rb,tbk->trk", row_hit, backward, precision=lax.Precision.HIGHEST
    )
    input_grad = input_grad.astype(jnp.bfloat16).reshape(
        micro_count, activations.shape[2], activations.shape[3]
    )
    ordered = jnp.take(input_grad, order, axis=0)
    received = passed_along(ordered, "section", -1)

    partial = jnp.einsum(
        "tbk,tbn->bkn", rows_in, act_cols, preferred_element_type=jnp.float32
    )
    held = partial.reshape((n_fsdp, blocks_dev) + (2,) * dp_bits + (chunk, block_size))
    for bit in range(dp_bits):
        axis_at = 2 + (dp_bits - 1 - bit)
        mine = (me_dp >> bit) & 1
        keep = lax.dynamic_index_in_dim(held, mine, axis_at, keepdims=False)
        send = lax.dynamic_index_in_dim(held, 1 - mine, axis_at, keepdims=False)
        held = keep + swapped(send, "dp", bit)
    owned = held[0]
    for k in range(1, n_fsdp):
        owned = owned + shifted(held[k], "fsdp", -k)
    full = butterfly_gather(owned, "dp", list(reversed(range(dp_bits))))
    full = full.reshape((n_dp, blocks_dev, chunk, block_size))
    full = jnp.transpose(full, (1, 0, 2, 3)).reshape(blocks_dev, block_size, block_size)
    grad_scale = jnp.sqrt(jnp.float32(tok_rows * n_fsdp * n_dp))
    return (received[None], (full / grad_scale)[None])


def solution(mesh):
    in_specs = (
        P("section", None, ("fsdp", "dp"), None),
        P("section", None, ("fsdp", "dp"), None),
        P("section", "fsdp", None, None),
        P("section", "fsdp", None),
        P(),
    )
    out_specs = (P("section", None, ("fsdp", "dp"), None), P("section", "fsdp", None, None))
    return jax.shard_map(local, mesh=mesh, in_specs=in_specs, out_specs=out_specs, check_vma=False)
```

```python
import math

import jax
import jax.numpy as jnp
from jax import lax
from jax.sharding import PartitionSpec as P


def passed_along(block, axis, distance):
    devices = range(lax.axis_size(axis))
    route = [(i - distance, i) for i in devices if i - distance in devices]
    return lax.ppermute(block, axis, route)


def shifted(x, axis, k):
    n = lax.axis_size(axis)
    return lax.ppermute(x, axis, [(i, (i + k) % n) for i in range(n)])


def swapped(x, axis, bit):
    n = lax.axis_size(axis)
    return lax.ppermute(x, axis, [(i, i ^ (1 << bit)) for i in range(n)])


def silu_slope(pre_act):
    sigmoid_val = jax.nn.sigmoid(pre_act)
    return sigmoid_val * (1.0 + pre_act * (1.0 - sigmoid_val))


def gather_over(x, axis):
    n = lax.axis_size(axis)
    return jnp.stack([x] + [shifted(x, axis, k) for k in range(1, n)])


def butterfly_gather(x, axis, bits):
    me = lax.axis_index(axis)
    held = x
    for bit in bits:
        other = swapped(held, axis, bit)
        mine_low = ((me >> bit) & 1) == 0
        held = jnp.where(mine_low, jnp.stack([held, other]), jnp.stack([other, held]))
    order = sorted(range(len(bits)), key=lambda a: -bits[len(bits) - 1 - a])
    perm = [order[i] for i in range(len(bits))] + list(range(len(bits), held.ndim))
    return jnp.transpose(held, perm)


def local(activations, out_grad, blocks, pattern, order):
    block_size = blocks.shape[-1]
    micro_count = activations.shape[1]
    tok_rows = activations.shape[1] * activations.shape[2]
    row_count = activations.shape[3] // block_size
    col_count = out_grad.shape[3] // block_size
    n_fsdp = lax.axis_size("fsdp")
    n_dp = lax.axis_size("dp")
    dp_bits = int(round(math.log2(n_dp)))
    assert 1 << dp_bits == n_dp and block_size % n_dp == 0
    chunk = block_size // n_dp
    me_dp = lax.axis_index("dp")

    own_blocks = blocks[0]
    blocks_dev = own_blocks.shape[0]

    assert n_fsdp % n_dp == 0
    per_dp = n_fsdp // n_dp
    weight_len = blocks_dev * block_size * block_size
    payload = jnp.concatenate(
        [own_blocks.reshape(-1), pattern[0].reshape(-1).astype(jnp.bfloat16)]
    )
    fetched = []
    for m in range(per_dp):
        pairs = []
        for f in range(n_fsdp):
            for d in range(n_dp):
                k = d + n_dp * m
                pairs.append((((f - k) % n_fsdp) * n_dp + d, f * n_dp + d))
        fetched.append(lax.ppermute(payload, ("fsdp", "dp"), pairs))
    fetched = jnp.stack(fetched)
    pieces = butterfly_gather(fetched, "dp", list(reversed(range(dp_bits))))
    pieces = pieces.reshape((n_dp, per_dp, -1))
    pieces = jnp.transpose(pieces, (1, 0, 2)).reshape(n_fsdp, -1)
    weights = pieces[:, :weight_len].reshape(n_fsdp * blocks_dev, block_size, block_size)
    all_indices = pieces[:, weight_len:].reshape(n_fsdp * blocks_dev, 2).astype(jnp.int32)

    features = activations[0].reshape(tok_rows, row_count, block_size)
    hidden_grad = out_grad[0].reshape(tok_rows, col_count, block_size)
    row_ids = all_indices[:, 0]
    col_ids = all_indices[:, 1]
    rows_in = jnp.take(features, row_ids, axis=1)
    product = jnp.einsum(
        "tbk,bkn->tbn", rows_in, weights, preferred_element_type=jnp.float32
    )
    same_col = (col_ids[:, None] == col_ids[None, :]).astype(jnp.float32)
    pre_act = jnp.einsum(
        "bc,tcn->tbn", same_col, product, precision=lax.Precision.HIGHEST
    )
    hidden_in = jnp.take(hidden_grad, col_ids, axis=1)
    act_cols = (hidden_in.astype(jnp.float32) * silu_slope(pre_act)).astype(jnp.bfloat16)

    backward = jnp.einsum(
        "tbn,bkn->tbk", act_cols, weights, preferred_element_type=jnp.float32
    )
    row_hit = (jnp.arange(row_count, dtype=jnp.int32)[:, None] == row_ids[None, :]).astype(
        jnp.float32
    )
    input_grad = jnp.einsum(
        "rb,tbk->trk", row_hit, backward, precision=lax.Precision.HIGHEST
    )
    arrived = passed_along(input_grad.astype(jnp.bfloat16), "section", -1)
    arrived = arrived.reshape(micro_count, activations.shape[2], activations.shape[3])
    received = jnp.take(arrived, order, axis=0)

    partial = jnp.einsum(
        "tbk,tbn->bkn", rows_in, act_cols, preferred_element_type=jnp.float32
    )
    held = partial.reshape((n_fsdp, blocks_dev) + (2,) * dp_bits + (chunk, block_size))
    for bit in range(dp_bits):
        axis_at = 2 + (dp_bits - 1 - bit)
        mine = (me_dp >> bit) & 1
        keep = lax.dynamic_index_in_dim(held, mine, axis_at, keepdims=False)
        send = lax.dynamic_index_in_dim(held, 1 - mine, axis_at, keepdims=False)
        held = keep + swapped(send, "dp", bit)
    owned = held[0]
    for k in range(1, n_fsdp):
        owned = owned + shifted(held[k], "fsdp", -k)
    full = butterfly_gather(owned, "dp", list(reversed(range(dp_bits))))
    full = full.reshape((n_dp, blocks_dev, chunk, block_size))
    full = jnp.transpose(full, (1, 0, 2, 3)).reshape(blocks_dev, block_size, block_size)
    grad_scale = jnp.sqrt(jnp.float32(tok_rows * n_fsdp * n_dp))
    return (received[None], (full / grad_scale)[None])


def solution(mesh):
    in_specs = (
        P("section", None, ("fsdp", "dp"), None),
        P("section", None, ("fsdp", "dp"), None),
        P("section", "fsdp", None, None),
        P("section", "fsdp", None),
        P(),
    )
    out_specs = (P("section", None, ("fsdp", "dp"), None), P("section", "fsdp", None, None))
    return jax.shard_map(local, mesh=mesh, in_specs=in_specs, out_specs=out_specs, check_vma=False)
```

```python
import math

import jax
import jax.numpy as jnp
from jax import lax
from jax.sharding import PartitionSpec as P


def passed_along(block, axis, distance):
    devices = range(lax.axis_size(axis))
    route = [(i - distance, i) for i in devices if i - distance in devices]
    return lax.ppermute(block, axis, route)


def shifted(x, axis, k):
    n = lax.axis_size(axis)
    return lax.ppermute(x, axis, [(i, (i + k) % n) for i in range(n)])


def swapped(x, axis, bit):
    n = lax.axis_size(axis)
    return lax.ppermute(x, axis, [(i, i ^ (1 << bit)) for i in range(n)])


def silu_slope(pre_act):
    sigmoid_val = jax.nn.sigmoid(pre_act)
    return sigmoid_val * (1.0 + pre_act * (1.0 - sigmoid_val))


def gather_over(x, axis):
    n = lax.axis_size(axis)
    return jnp.stack([x] + [shifted(x, axis, k) for k in range(1, n)])


def butterfly_gather(x, axis, bits):
    me = lax.axis_index(axis)
    held = x
    for bit in bits:
        other = swapped(held, axis, bit)
        mine_low = ((me >> bit) & 1) == 0
        held = jnp.where(mine_low, jnp.stack([held, other]), jnp.stack([other, held]))
    order = sorted(range(len(bits)), key=lambda a: -bits[len(bits) - 1 - a])
    perm = [order[i] for i in range(len(bits))] + list(range(len(bits), held.ndim))
    return jnp.transpose(held, perm)


def local(activations, out_grad, blocks, pattern, order):
    block_size = blocks.shape[-1]
    micro_count = activations.shape[1]
    tok_rows = activations.shape[1] * activations.shape[2]
    row_count = activations.shape[3] // block_size
    col_count = out_grad.shape[3] // block_size
    n_fsdp = lax.axis_size("fsdp")
    n_dp = lax.axis_size("dp")
    dp_bits = int(round(math.log2(n_dp)))
    assert 1 << dp_bits == n_dp and block_size % n_dp == 0
    chunk = block_size // n_dp
    me_dp = lax.axis_index("dp")

    own_blocks = blocks[0]
    blocks_dev = own_blocks.shape[0]

    assert n_fsdp % n_dp == 0
    per_dp = n_fsdp // n_dp
    weight_len = blocks_dev * block_size * block_size
    payload = jnp.concatenate(
        [own_blocks.reshape(-1), pattern[0].reshape(-1).astype(jnp.bfloat16)]
    )
    fetched = []
    for m in range(per_dp):
        pairs = []
        for f in range(n_fsdp):
            for d in range(n_dp):
                k = d + n_dp * m
                pairs.append((((f - k) % n_fsdp) * n_dp + d, f * n_dp + d))
        fetched.append(lax.ppermute(payload, ("fsdp", "dp"), pairs))
    fetched = jnp.stack(fetched)
    pieces = butterfly_gather(fetched, "dp", list(reversed(range(dp_bits))))
    pieces = pieces.reshape((n_dp, per_dp, -1))
    pieces = jnp.transpose(pieces, (1, 0, 2)).reshape(n_fsdp, -1)
    weights = pieces[:, :weight_len].reshape(n_fsdp * blocks_dev, block_size, block_size)
    all_indices = pieces[:, weight_len:].reshape(n_fsdp * blocks_dev, 2).astype(jnp.int32)

    features = activations[0].reshape(tok_rows, row_count, block_size)
    hidden_grad = out_grad[0].reshape(tok_rows, col_count, block_size)
    row_ids = all_indices[:, 0]
    col_ids = all_indices[:, 1]
    rows_in = jnp.take(features, row_ids, axis=1)
    product = jnp.einsum(
        "tbk,bkn->tbn", rows_in, weights, preferred_element_type=jnp.float32
    )
    same_col = (col_ids[:, None] == col_ids[None, :]).astype(jnp.float32)
    pre_act = jnp.einsum(
        "bc,tcn->tbn", same_col, product, precision=lax.Precision.HIGHEST
    )
    hidden_in = jnp.take(hidden_grad, col_ids, axis=1)
    act_cols = (hidden_in.astype(jnp.float32) * silu_slope(pre_act)).astype(jnp.bfloat16)

    backward = jnp.einsum(
        "tbn,bkn->tbk", act_cols, weights, preferred_element_type=jnp.float32
    )
    row_hit = (jnp.arange(row_count, dtype=jnp.int32)[:, None] == row_ids[None, :]).astype(
        jnp.float32
    )
    input_grad = jnp.einsum(
        "rb,tbk->trk", row_hit, backward, precision=lax.Precision.HIGHEST
    )
    arrived = passed_along(input_grad.astype(jnp.bfloat16), "section", -1)
    arrived = arrived.reshape(micro_count, activations.shape[2], activations.shape[3])
    received = jnp.take(arrived, order, axis=0)

    partial = jnp.einsum(
        "tbk,tbn->bkn", rows_in, act_cols, preferred_element_type=jnp.float32
    )
    held = partial.reshape((n_fsdp, blocks_dev) + (2,) * dp_bits + (chunk, block_size))
    for bit in range(dp_bits):
        axis_at = 2 + (dp_bits - 1 - bit)
        mine = (me_dp >> bit) & 1
        keep = lax.dynamic_index_in_dim(held, mine, axis_at, keepdims=False)
        send = lax.dynamic_index_in_dim(held, 1 - mine, axis_at, keepdims=False)
        if bit == 0:
            held = keep + swapped(send, "dp", bit)
        else:
            held = keep + swapped(send.astype(jnp.bfloat16), "dp", bit).astype(jnp.float32)
    owned = held[0]
    for k in range(1, n_fsdp):
        owned = owned + shifted(held[k].astype(jnp.bfloat16), "fsdp", -k).astype(jnp.float32)
    full = butterfly_gather(owned, "dp", list(reversed(range(dp_bits))))
    full = full.reshape((n_dp, blocks_dev, chunk, block_size))
    full = jnp.transpose(full, (1, 0, 2, 3)).reshape(blocks_dev, block_size, block_size)
    grad_scale = jnp.sqrt(jnp.float32(tok_rows * n_fsdp * n_dp))
    return (received[None], (full / grad_scale)[None])


def solution(mesh):
    in_specs = (
        P("section", None, ("fsdp", "dp"), None),
        P("section", None, ("fsdp", "dp"), None),
        P("section", "fsdp", None, None),
        P("section", "fsdp", None),
        P(),
    )
    out_specs = (P("section", None, ("fsdp", "dp"), None), P("section", "fsdp", None, None))
    return jax.shard_map(local, mesh=mesh, in_specs=in_specs, out_specs=out_specs, check_vma=False)
```

```python
import math

import jax
import jax.numpy as jnp
from jax import lax
from jax.experimental import pallas as pl
from jax.experimental.pallas import tpu as pltpu
from jax.sharding import PartitionSpec as P


def passed_along(block, axis, distance):
    devices = range(lax.axis_size(axis))
    route = [(i - distance, i) for i in devices if i - distance in devices]
    return lax.ppermute(block, axis, route)


def shifted(x, axis, k):
    n = lax.axis_size(axis)
    return lax.ppermute(x, axis, [(i, (i + k) % n) for i in range(n)])


def swapped(x, axis, bit):
    n = lax.axis_size(axis)
    return lax.ppermute(x, axis, [(i, i ^ (1 << bit)) for i in range(n)])


def silu_slope(pre_act):
    sigmoid_val = jax.nn.sigmoid(pre_act)
    return sigmoid_val * (1.0 + pre_act * (1.0 - sigmoid_val))


def block_kernel(rows_ref, cols_ref, rep_ref, feat_hbm, hid_hbm, w_ref, ig_ref, pg_ref,
                 xs, hs, pr, acc, sems):
    block_count = w_ref.shape[0]
    width = w_ref.shape[-1]

    def copies(b):
        r = pl.multiple_of(rows_ref[b] * width, width)
        c = pl.multiple_of(cols_ref[b] * width, width)
        return (
            pltpu.make_async_copy(feat_hbm.at[:, pl.ds(r, width)], xs.at[b], sems.at[0, b]),
            pltpu.make_async_copy(hid_hbm.at[:, pl.ds(c, width)], hs.at[b], sems.at[1, b]),
        )

    @pl.loop(0, block_count)
    def _(b):
        for cp in copies(b):
            cp.start()

    acc[...] = jnp.zeros(acc.shape, acc.dtype)

    @pl.loop(0, block_count)
    def _(b):
        for cp in copies(b):
            cp.wait()
        pr[b] = jnp.dot(xs[b], w_ref[b], preferred_element_type=jnp.float32)

    @pl.loop(0, block_count)
    def _(b):
        first = rep_ref[b]

        @pl.when(first != b)
        def _():
            pr[first] = pr[first] + pr[b]

    @pl.loop(0, block_count)
    def _(b):
        pre_act = pr[rep_ref[b]]
        act = (hs[b].astype(jnp.float32) * silu_slope(pre_act)).astype(jnp.bfloat16)
        back = lax.dot_general(
            act, w_ref[b], (((1,), (1,)), ((), ())), preferred_element_type=jnp.float32
        )
        row = rows_ref[b]
        acc[row] = acc[row] + back
        pg_ref[b] = lax.dot_general(
            xs[b], act, (((0,), (0,)), ((), ())), preferred_element_type=jnp.float32
        )

    ig_ref[...] = acc[...].astype(ig_ref.dtype)


def block_pass(features, hidden_grad, weights, row_ids, col_ids, row_count):
    tokens = features.shape[0]
    block_count, width, _ = weights.shape
    same = col_ids[:, None] == col_ids[None, :]
    first = jnp.argmax(same, axis=1).astype(jnp.int32)
    smem = pl.BlockSpec(memory_space=pltpu.SMEM)
    anyspace = pl.BlockSpec(memory_space=pl.ANY)
    vmem = pl.BlockSpec(memory_space=pltpu.VMEM)
    return pl.pallas_call(
        block_kernel,
        out_shape=(
            jax.ShapeDtypeStruct((row_count, tokens, width), jnp.bfloat16),
            jax.ShapeDtypeStruct((block_count, width, width), jnp.float32),
        ),
        in_specs=[smem, smem, smem, anyspace, anyspace, vmem],
        out_specs=(vmem, vmem),
        scratch_shapes=[
            pltpu.VMEM((block_count, tokens, width), jnp.bfloat16),
            pltpu.VMEM((block_count, tokens, width), jnp.bfloat16),
            pltpu.VMEM((block_count, tokens, width), jnp.float32),
            pltpu.VMEM((row_count, tokens, width), jnp.float32),
            pltpu.SemaphoreType.DMA((2, block_count)),
        ],
        cost_estimate=pl.CostEstimate(
            flops=6 * block_count * tokens * width * width,
            transcendentals=block_count * tokens * width,
            bytes_accessed=block_count * width * (4 * tokens + 6 * width)
            + row_count * tokens * width * 2,
        ),
    )(row_ids, col_ids, first, features, hidden_grad, weights)


def gather_over(x, axis):
    n = lax.axis_size(axis)
    return jnp.stack([x] + [shifted(x, axis, k) for k in range(1, n)])


def butterfly_gather(x, axis, bits):
    me = lax.axis_index(axis)
    held = x
    for bit in bits:
        other = swapped(held, axis, bit)
        mine_low = ((me >> bit) & 1) == 0
        held = jnp.where(mine_low, jnp.stack([held, other]), jnp.stack([other, held]))
    order = sorted(range(len(bits)), key=lambda a: -bits[len(bits) - 1 - a])
    perm = [order[i] for i in range(len(bits))] + list(range(len(bits), held.ndim))
    return jnp.transpose(held, perm)


def local(activations, out_grad, blocks, pattern, order):
    block_size = blocks.shape[-1]
    micro_count = activations.shape[1]
    tok_rows = activations.shape[1] * activations.shape[2]
    row_count = activations.shape[3] // block_size
    col_count = out_grad.shape[3] // block_size
    n_fsdp = lax.axis_size("fsdp")
    n_dp = lax.axis_size("dp")
    dp_bits = int(round(math.log2(n_dp)))
    assert 1 << dp_bits == n_dp and block_size % n_dp == 0
    chunk = block_size // n_dp
    me_dp = lax.axis_index("dp")

    own_blocks = blocks[0]
    blocks_dev = own_blocks.shape[0]

    assert n_fsdp % n_dp == 0
    per_dp = n_fsdp // n_dp
    weight_len = blocks_dev * block_size * block_size
    payload = jnp.concatenate(
        [own_blocks.reshape(-1), pattern[0].reshape(-1).astype(jnp.bfloat16)]
    )
    fetched = []
    for m in range(per_dp):
        pairs = []
        for f in range(n_fsdp):
            for d in range(n_dp):
                k = d + n_dp * m
                pairs.append((((f - k) % n_fsdp) * n_dp + d, f * n_dp + d))
        fetched.append(lax.ppermute(payload, ("fsdp", "dp"), pairs))
    fetched = jnp.stack(fetched)
    pieces = butterfly_gather(fetched, "dp", list(reversed(range(dp_bits))))
    pieces = pieces.reshape((n_dp, per_dp, -1))
    pieces = jnp.transpose(pieces, (1, 0, 2)).reshape(n_fsdp, -1)
    weights = pieces[:, :weight_len].reshape(n_fsdp * blocks_dev, block_size, block_size)
    all_indices = pieces[:, weight_len:].reshape(n_fsdp * blocks_dev, 2).astype(jnp.int32)

    row_ids = all_indices[:, 0]
    col_ids = all_indices[:, 1]
    input_grad, partial = block_pass(
        activations[0].reshape(tok_rows, -1),
        out_grad[0].reshape(tok_rows, -1),
        weights,
        row_ids,
        col_ids,
        row_count,
    )
    arrived = passed_along(input_grad, "section", -1)
    arrived = jnp.transpose(arrived, (1, 0, 2)).reshape(
        micro_count, activations.shape[2], activations.shape[3]
    )
    received = jnp.take(arrived, order, axis=0)

    held = partial.reshape((n_fsdp, blocks_dev) + (2,) * dp_bits + (chunk, block_size))
    for bit in range(dp_bits):
        axis_at = 2 + (dp_bits - 1 - bit)
        mine = (me_dp >> bit) & 1
        keep = lax.dynamic_index_in_dim(held, mine, axis_at, keepdims=False)
        send = lax.dynamic_index_in_dim(held, 1 - mine, axis_at, keepdims=False)
        if bit == 0:
            held = keep + swapped(send, "dp", bit)
        else:
            held = keep + swapped(send.astype(jnp.bfloat16), "dp", bit).astype(jnp.float32)
    owned = held[0]
    for k in range(1, n_fsdp):
        owned = owned + shifted(held[k].astype(jnp.bfloat16), "fsdp", -k).astype(jnp.float32)
    full = butterfly_gather(owned, "dp", list(reversed(range(dp_bits))))
    full = full.reshape((n_dp, blocks_dev, chunk, block_size))
    full = jnp.transpose(full, (1, 0, 2, 3)).reshape(blocks_dev, block_size, block_size)
    grad_scale = jnp.sqrt(jnp.float32(tok_rows * n_fsdp * n_dp))
    return (received[None], (full / grad_scale)[None])


def solution(mesh):
    in_specs = (
        P("section", None, ("fsdp", "dp"), None),
        P("section", None, ("fsdp", "dp"), None),
        P("section", "fsdp", None, None),
        P("section", "fsdp", None),
        P(),
    )
    out_specs = (P("section", None, ("fsdp", "dp"), None), P("section", "fsdp", None, None))
    return jax.shard_map(local, mesh=mesh, in_specs=in_specs, out_specs=out_specs, check_vma=False)
```

```python
import math

import jax
import jax.numpy as jnp
from jax import lax
from jax.experimental import pallas as pl
from jax.experimental.pallas import tpu as pltpu
from jax.sharding import PartitionSpec as P


def passed_along(block, axis, distance):
    devices = range(lax.axis_size(axis))
    route = [(i - distance, i) for i in devices if i - distance in devices]
    return lax.ppermute(block, axis, route)


def shifted(x, axis, k):
    n = lax.axis_size(axis)
    return lax.ppermute(x, axis, [(i, (i + k) % n) for i in range(n)])


def swapped(x, axis, bit):
    n = lax.axis_size(axis)
    return lax.ppermute(x, axis, [(i, i ^ (1 << bit)) for i in range(n)])


def silu_slope(pre_act):
    sigmoid_val = jax.nn.sigmoid(pre_act)
    return sigmoid_val * (1.0 + pre_act * (1.0 - sigmoid_val))


def block_kernel(rows_ref, cols_ref, rep_ref, feat_hbm, hid_hbm, w_ref, ig_ref, pg_ref,
                 xs, hs, pr, acc, sems):
    block_count = w_ref.shape[0]
    width = w_ref.shape[-1]

    def copies(b):
        r = pl.multiple_of(rows_ref[b] * width, width)
        c = pl.multiple_of(cols_ref[b] * width, width)
        return (
            pltpu.make_async_copy(feat_hbm.at[:, pl.ds(r, width)], xs.at[b], sems.at[0, b]),
            pltpu.make_async_copy(hid_hbm.at[:, pl.ds(c, width)], hs.at[b], sems.at[1, b]),
        )

    @pl.loop(0, block_count)
    def _(b):
        for cp in copies(b):
            cp.start()

    acc[...] = jnp.zeros(acc.shape, acc.dtype)

    @pl.loop(0, block_count)
    def _(b):
        for cp in copies(b):
            cp.wait()
        pr[b] = jnp.dot(xs[b], w_ref[b], preferred_element_type=jnp.float32)

    @pl.loop(0, block_count)
    def _(b):
        first = rep_ref[b]

        @pl.when(first != b)
        def _():
            pr[first] = pr[first] + pr[b]

    @pl.loop(0, block_count)
    def _(b):
        pre_act = pr[rep_ref[b]]
        act = (hs[b].astype(jnp.float32) * silu_slope(pre_act)).astype(jnp.bfloat16)
        back = lax.dot_general(
            act, w_ref[b], (((1,), (1,)), ((), ())), preferred_element_type=jnp.float32
        )
        row = rows_ref[b]
        acc[row] = acc[row] + back
        pg_ref[b] = lax.dot_general(
            xs[b], act, (((0,), (0,)), ((), ())), preferred_element_type=jnp.float32
        )

    ig_ref[...] = acc[...].astype(ig_ref.dtype)


def block_pass(features, hidden_grad, weights, row_ids, col_ids, row_count):
    tokens = features.shape[0]
    block_count, width, _ = weights.shape
    same = col_ids[:, None] == col_ids[None, :]
    first = jnp.argmax(same, axis=1).astype(jnp.int32)
    smem = pl.BlockSpec(memory_space=pltpu.SMEM)
    anyspace = pl.BlockSpec(memory_space=pl.ANY)
    vmem = pl.BlockSpec(memory_space=pltpu.VMEM)
    return pl.pallas_call(
        block_kernel,
        out_shape=(
            jax.ShapeDtypeStruct((row_count, tokens, width), jnp.bfloat16),
            jax.ShapeDtypeStruct((block_count, width, width), jnp.float32),
        ),
        in_specs=[smem, smem, smem, anyspace, anyspace, vmem],
        out_specs=(vmem, vmem),
        scratch_shapes=[
            pltpu.VMEM((block_count, tokens, width), jnp.bfloat16),
            pltpu.VMEM((block_count, tokens, width), jnp.bfloat16),
            pltpu.VMEM((block_count, tokens, width), jnp.float32),
            pltpu.VMEM((row_count, tokens, width), jnp.float32),
            pltpu.SemaphoreType.DMA((2, block_count)),
        ],
        cost_estimate=pl.CostEstimate(
            flops=6 * block_count * tokens * width * width,
            transcendentals=block_count * tokens * width,
            bytes_accessed=block_count * width * (4 * tokens + 6 * width)
            + row_count * tokens * width * 2,
        ),
    )(row_ids, col_ids, first, features, hidden_grad, weights)


def gather_over(x, axis):
    n = lax.axis_size(axis)
    return jnp.stack([x] + [shifted(x, axis, k) for k in range(1, n)])


def butterfly_gather(x, axis, bits):
    me = lax.axis_index(axis)
    held = x
    for bit in bits:
        other = swapped(held, axis, bit)
        mine_low = ((me >> bit) & 1) == 0
        held = jnp.where(mine_low, jnp.stack([held, other]), jnp.stack([other, held]))
    order = sorted(range(len(bits)), key=lambda a: -bits[len(bits) - 1 - a])
    perm = [order[i] for i in range(len(bits))] + list(range(len(bits), held.ndim))
    return jnp.transpose(held, perm)


def local(activations, out_grad, blocks, pattern, order):
    block_size = blocks.shape[-1]
    micro_count = activations.shape[1]
    tok_rows = activations.shape[1] * activations.shape[2]
    row_count = activations.shape[3] // block_size
    col_count = out_grad.shape[3] // block_size
    n_fsdp = lax.axis_size("fsdp")
    n_dp = lax.axis_size("dp")
    dp_bits = int(round(math.log2(n_dp)))
    assert 1 << dp_bits == n_dp and block_size % n_dp == 0
    chunk = block_size // n_dp
    me_dp = lax.axis_index("dp")

    own_blocks = blocks[0]
    blocks_dev = own_blocks.shape[0]

    assert n_fsdp % n_dp == 0
    per_dp = n_fsdp // n_dp
    weight_len = blocks_dev * block_size * block_size
    payload = jnp.concatenate(
        [own_blocks.reshape(-1), pattern[0].reshape(-1).astype(jnp.bfloat16)]
    )
    fetched = []
    for m in range(per_dp):
        pairs = []
        for f in range(n_fsdp):
            for d in range(n_dp):
                k = d + n_dp * m
                pairs.append((((f - k) % n_fsdp) * n_dp + d, f * n_dp + d))
        fetched.append(lax.ppermute(payload, ("fsdp", "dp"), pairs))
    fetched = jnp.stack(fetched)
    pieces = butterfly_gather(fetched, "dp", list(reversed(range(dp_bits))))
    pieces = pieces.reshape((n_dp, per_dp, -1))
    pieces = jnp.transpose(pieces, (1, 0, 2)).reshape(n_fsdp, -1)
    weights = pieces[:, :weight_len].reshape(n_fsdp * blocks_dev, block_size, block_size)
    all_indices = pieces[:, weight_len:].reshape(n_fsdp * blocks_dev, 2).astype(jnp.int32)

    row_ids = all_indices[:, 0]
    col_ids = all_indices[:, 1]
    input_grad, partial = block_pass(
        activations[0].reshape(tok_rows, -1),
        out_grad[0].reshape(tok_rows, -1),
        weights,
        row_ids,
        col_ids,
        row_count,
    )
    block_count = row_ids.shape[0]
    if block_count < row_count:
        hit = jnp.take(input_grad, row_ids, axis=0)
        payload = jnp.concatenate([hit.reshape(-1), row_ids.astype(jnp.bfloat16)])
        payload = passed_along(payload, "section", -1)
        got_rows = payload[hit.size:].astype(jnp.int32)
        got = payload[: hit.size].reshape(hit.shape)
        arrived = jnp.zeros_like(input_grad).at[got_rows].set(got)
    else:
        arrived = passed_along(input_grad, "section", -1)
    arrived = jnp.transpose(arrived, (1, 0, 2)).reshape(
        micro_count, activations.shape[2], activations.shape[3]
    )
    received = jnp.take(arrived, order, axis=0)

    held = partial.reshape((n_fsdp, blocks_dev) + (2,) * dp_bits + (chunk, block_size))
    for bit in range(dp_bits):
        axis_at = 2 + (dp_bits - 1 - bit)
        mine = (me_dp >> bit) & 1
        keep = lax.dynamic_index_in_dim(held, mine, axis_at, keepdims=False)
        send = lax.dynamic_index_in_dim(held, 1 - mine, axis_at, keepdims=False)
        if bit == 0:
            held = keep + swapped(send, "dp", bit)
        else:
            held = keep + swapped(send.astype(jnp.bfloat16), "dp", bit).astype(jnp.float32)
    owned = held[0]
    for k in range(1, n_fsdp):
        owned = owned + shifted(held[k].astype(jnp.bfloat16), "fsdp", -k).astype(jnp.float32)
    full = butterfly_gather(owned, "dp", list(reversed(range(dp_bits))))
    full = full.reshape((n_dp, blocks_dev, chunk, block_size))
    full = jnp.transpose(full, (1, 0, 2, 3)).reshape(blocks_dev, block_size, block_size)
    grad_scale = jnp.sqrt(jnp.float32(tok_rows * n_fsdp * n_dp))
    return (received[None], (full / grad_scale)[None])


def solution(mesh):
    in_specs = (
        P("section", None, ("fsdp", "dp"), None),
        P("section", None, ("fsdp", "dp"), None),
        P("section", "fsdp", None, None),
        P("section", "fsdp", None),
        P(),
    )
    out_specs = (P("section", None, ("fsdp", "dp"), None), P("section", "fsdp", None, None))
    return jax.shard_map(local, mesh=mesh, in_specs=in_specs, out_specs=out_specs, check_vma=False)
```

```python
import math

import jax
import jax.numpy as jnp
from jax import lax
from jax.experimental import pallas as pl
from jax.experimental.pallas import tpu as pltpu
from jax.sharding import PartitionSpec as P


def passed_along(block, axis, distance):
    devices = range(lax.axis_size(axis))
    route = [(i - distance, i) for i in devices if i - distance in devices]
    return lax.ppermute(block, axis, route)


def shifted(x, axis, k):
    n = lax.axis_size(axis)
    return lax.ppermute(x, axis, [(i, (i + k) % n) for i in range(n)])


def swapped(x, axis, bit):
    n = lax.axis_size(axis)
    return lax.ppermute(x, axis, [(i, i ^ (1 << bit)) for i in range(n)])


def silu_slope(pre_act):
    sigmoid_val = jax.nn.sigmoid(pre_act)
    return sigmoid_val * (1.0 + pre_act * (1.0 - sigmoid_val))


def block_kernel(rows_ref, cols_ref, rep_ref, feat_hbm, hid_hbm, w_ref, ig_ref, pg_ref,
                 xs, hs, pr, acc, sems):
    block_count = w_ref.shape[0]
    width = w_ref.shape[-1]

    def copies(b):
        r = pl.multiple_of(rows_ref[b] * width, width)
        c = pl.multiple_of(cols_ref[b] * width, width)
        return (
            pltpu.make_async_copy(feat_hbm.at[:, pl.ds(r, width)], xs.at[b], sems.at[0, b]),
            pltpu.make_async_copy(hid_hbm.at[:, pl.ds(c, width)], hs.at[b], sems.at[1, b]),
        )

    @pl.loop(0, block_count)
    def _(b):
        for cp in copies(b):
            cp.start()

    acc[...] = jnp.zeros(acc.shape, acc.dtype)

    @pl.loop(0, block_count)
    def _(b):
        for cp in copies(b):
            cp.wait()
        pr[b] = jnp.dot(xs[b], w_ref[b], preferred_element_type=jnp.float32)

    @pl.loop(0, block_count)
    def _(b):
        first = rep_ref[b]

        @pl.when(first != b)
        def _():
            pr[first] = pr[first] + pr[b]

    @pl.loop(0, block_count)
    def _(b):
        pre_act = pr[rep_ref[b]]
        act = (hs[b].astype(jnp.float32) * silu_slope(pre_act)).astype(jnp.bfloat16)
        back = lax.dot_general(
            act, w_ref[b], (((1,), (1,)), ((), ())), preferred_element_type=jnp.float32
        )
        row = rows_ref[b]
        acc[row] = acc[row] + back
        pg_ref[b] = lax.dot_general(
            xs[b], act, (((0,), (0,)), ((), ())), preferred_element_type=jnp.float32
        )

    ig_ref[...] = acc[...].astype(ig_ref.dtype)


def block_pass(features, hidden_grad, weights, row_ids, col_ids, row_count):
    tokens = features.shape[0]
    block_count, width, _ = weights.shape
    same = col_ids[:, None] == col_ids[None, :]
    first = jnp.argmax(same, axis=1).astype(jnp.int32)
    smem = pl.BlockSpec(memory_space=pltpu.SMEM)
    anyspace = pl.BlockSpec(memory_space=pl.ANY)
    vmem = pl.BlockSpec(memory_space=pltpu.VMEM)
    return pl.pallas_call(
        block_kernel,
        out_shape=(
            jax.ShapeDtypeStruct((row_count, tokens, width), jnp.bfloat16),
            jax.ShapeDtypeStruct((block_count, width, width), jnp.float32),
        ),
        in_specs=[smem, smem, smem, anyspace, anyspace, vmem],
        out_specs=(vmem, vmem),
        scratch_shapes=[
            pltpu.VMEM((block_count, tokens, width), jnp.bfloat16),
            pltpu.VMEM((block_count, tokens, width), jnp.bfloat16),
            pltpu.VMEM((block_count, tokens, width), jnp.float32),
            pltpu.VMEM((row_count, tokens, width), jnp.float32),
            pltpu.SemaphoreType.DMA((2, block_count)),
        ],
        cost_estimate=pl.CostEstimate(
            flops=6 * block_count * tokens * width * width,
            transcendentals=block_count * tokens * width,
            bytes_accessed=block_count * width * (4 * tokens + 6 * width)
            + row_count * tokens * width * 2,
        ),
    )(row_ids, col_ids, first, features, hidden_grad, weights)


def gather_over(x, axis):
    n = lax.axis_size(axis)
    return jnp.stack([x] + [shifted(x, axis, k) for k in range(1, n)])


def butterfly_gather(x, axis, bits):
    me = lax.axis_index(axis)
    held = x
    for bit in bits:
        other = swapped(held, axis, bit)
        mine_low = ((me >> bit) & 1) == 0
        held = jnp.where(mine_low, jnp.stack([held, other]), jnp.stack([other, held]))
    order = sorted(range(len(bits)), key=lambda a: -bits[len(bits) - 1 - a])
    perm = [order[i] for i in range(len(bits))] + list(range(len(bits), held.ndim))
    return jnp.transpose(held, perm)


def local(activations, out_grad, blocks, pattern, order):
    block_size = blocks.shape[-1]
    micro_count = activations.shape[1]
    tok_rows = activations.shape[1] * activations.shape[2]
    row_count = activations.shape[3] // block_size
    col_count = out_grad.shape[3] // block_size
    n_fsdp = lax.axis_size("fsdp")
    n_dp = lax.axis_size("dp")
    dp_bits = int(round(math.log2(n_dp)))
    assert 1 << dp_bits == n_dp and block_size % n_dp == 0
    chunk = block_size // n_dp
    me_dp = lax.axis_index("dp")

    own_blocks = blocks[0]
    blocks_dev = own_blocks.shape[0]

    assert n_fsdp % n_dp == 0
    per_dp = n_fsdp // n_dp
    weight_rows = blocks_dev * block_size
    assert 2 * blocks_dev <= block_size
    index_tile = jnp.zeros((16, block_size), jnp.bfloat16)
    index_tile = index_tile.at[0, : 2 * blocks_dev].set(
        pattern[0].reshape(-1).astype(jnp.bfloat16)
    )
    payload = jnp.concatenate([own_blocks.reshape(weight_rows, block_size), index_tile])
    fetched = []
    for m in range(per_dp):
        pairs = []
        for f in range(n_fsdp):
            for d in range(n_dp):
                k = d + n_dp * m
                pairs.append((((f - k) % n_fsdp) * n_dp + d, f * n_dp + d))
        fetched.append(lax.ppermute(payload, ("fsdp", "dp"), pairs))
    fetched = jnp.stack(fetched)
    pieces = butterfly_gather(fetched, "dp", list(reversed(range(dp_bits))))
    pieces = pieces.reshape((n_dp, per_dp) + payload.shape)
    pieces = jnp.transpose(pieces, (1, 0, 2, 3)).reshape((n_fsdp,) + payload.shape)
    weights = pieces[:, :weight_rows].reshape(n_fsdp * blocks_dev, block_size, block_size)
    all_indices = (
        pieces[:, weight_rows, : 2 * blocks_dev]
        .reshape(n_fsdp * blocks_dev, 2)
        .astype(jnp.int32)
    )

    row_ids = all_indices[:, 0]
    col_ids = all_indices[:, 1]
    input_grad, partial = block_pass(
        activations[0].reshape(tok_rows, -1),
        out_grad[0].reshape(tok_rows, -1),
        weights,
        row_ids,
        col_ids,
        row_count,
    )
    block_count = row_ids.shape[0]
    if block_count < row_count:
        hit = jnp.take(input_grad, row_ids, axis=0)
        payload = jnp.concatenate([hit.reshape(-1), row_ids.astype(jnp.bfloat16)])
        payload = passed_along(payload, "section", -1)
        got_rows = payload[hit.size:].astype(jnp.int32)
        got = payload[: hit.size].reshape(hit.shape)
        arrived = jnp.zeros_like(input_grad).at[got_rows].set(got)
    else:
        arrived = passed_along(input_grad, "section", -1)
    arrived = jnp.transpose(arrived, (1, 0, 2)).reshape(
        micro_count, activations.shape[2], activations.shape[3]
    )
    received = jnp.take(arrived, order, axis=0)

    held = partial.reshape((n_fsdp, blocks_dev) + (2,) * dp_bits + (chunk, block_size))
    for bit in range(dp_bits):
        axis_at = 2 + (dp_bits - 1 - bit)
        mine = (me_dp >> bit) & 1
        keep = lax.dynamic_index_in_dim(held, mine, axis_at, keepdims=False)
        send = lax.dynamic_index_in_dim(held, 1 - mine, axis_at, keepdims=False)
        if bit == 0:
            held = keep + swapped(send, "dp", bit)
        else:
            held = keep + swapped(send.astype(jnp.bfloat16), "dp", bit).astype(jnp.float32)
    owned = held[0]
    for k in range(1, n_fsdp):
        owned = owned + shifted(held[k].astype(jnp.bfloat16), "fsdp", -k).astype(jnp.float32)
    full = butterfly_gather(owned, "dp", list(reversed(range(dp_bits))))
    full = full.reshape((n_dp, blocks_dev, chunk, block_size))
    full = jnp.transpose(full, (1, 0, 2, 3)).reshape(blocks_dev, block_size, block_size)
    grad_scale = jnp.sqrt(jnp.float32(tok_rows * n_fsdp * n_dp))
    return (received[None], (full / grad_scale)[None])


def solution(mesh):
    in_specs = (
        P("section", None, ("fsdp", "dp"), None),
        P("section", None, ("fsdp", "dp"), None),
        P("section", "fsdp", None, None),
        P("section", "fsdp", None),
        P(),
    )
    out_specs = (P("section", None, ("fsdp", "dp"), None), P("section", "fsdp", None, None))
    return jax.shard_map(local, mesh=mesh, in_specs=in_specs, out_specs=out_specs, check_vma=False)
```

```python
import math

import jax
import jax.numpy as jnp
from jax import lax
from jax.experimental import pallas as pl
from jax.experimental.pallas import tpu as pltpu
from jax.sharding import PartitionSpec as P


def passed_along(block, axis, distance):
    devices = range(lax.axis_size(axis))
    route = [(i - distance, i) for i in devices if i - distance in devices]
    return lax.ppermute(block, axis, route)


def shifted(x, axis, k):
    n = lax.axis_size(axis)
    return lax.ppermute(x, axis, [(i, (i + k) % n) for i in range(n)])


def swapped(x, axis, bit):
    n = lax.axis_size(axis)
    return lax.ppermute(x, axis, [(i, i ^ (1 << bit)) for i in range(n)])


def silu_slope(pre_act):
    sigmoid_val = jax.nn.sigmoid(pre_act)
    return sigmoid_val * (1.0 + pre_act * (1.0 - sigmoid_val))


def block_kernel(rows_ref, cols_ref, rep_ref, feat_hbm, hid_hbm, w_ref, ig_ref, pg_ref,
                 xs, hs, pr, acc, sems):
    block_count = w_ref.shape[0]
    width = w_ref.shape[-1]

    def copies(b):
        r = pl.multiple_of(rows_ref[b] * width, width)
        c = pl.multiple_of(cols_ref[b] * width, width)
        return (
            pltpu.make_async_copy(feat_hbm.at[:, pl.ds(r, width)], xs.at[b], sems.at[0, b]),
            pltpu.make_async_copy(hid_hbm.at[:, pl.ds(c, width)], hs.at[b], sems.at[1, b]),
        )

    @pl.loop(0, block_count)
    def _(b):
        for cp in copies(b):
            cp.start()

    acc[...] = jnp.zeros(acc.shape, acc.dtype)

    @pl.loop(0, block_count)
    def _(b):
        for cp in copies(b):
            cp.wait()
        pr[b] = jnp.dot(xs[b], w_ref[b], preferred_element_type=jnp.float32)

    @pl.loop(0, block_count)
    def _(b):
        first = rep_ref[b]

        @pl.when(first != b)
        def _():
            pr[first] = pr[first] + pr[b]

    @pl.loop(0, block_count)
    def _(b):
        pre_act = pr[rep_ref[b]]
        act = (hs[b].astype(jnp.float32) * silu_slope(pre_act)).astype(jnp.bfloat16)
        back = lax.dot_general(
            act, w_ref[b], (((1,), (1,)), ((), ())), preferred_element_type=jnp.float32
        )
        row = rows_ref[b]
        acc[row] = acc[row] + back
        pg_ref[b] = lax.dot_general(
            xs[b], act, (((0,), (0,)), ((), ())), preferred_element_type=jnp.float32
        )

    ig_ref[...] = acc[...].astype(ig_ref.dtype)


def block_pass(features, hidden_grad, weights, row_ids, col_ids, row_count):
    tokens = features.shape[0]
    block_count, width, _ = weights.shape
    same = col_ids[:, None] == col_ids[None, :]
    first = jnp.argmax(same, axis=1).astype(jnp.int32)
    smem = pl.BlockSpec(memory_space=pltpu.SMEM)
    anyspace = pl.BlockSpec(memory_space=pl.ANY)
    vmem = pl.BlockSpec(memory_space=pltpu.VMEM)
    return pl.pallas_call(
        block_kernel,
        out_shape=(
            jax.ShapeDtypeStruct((row_count, tokens, width), jnp.bfloat16),
            jax.ShapeDtypeStruct((block_count, width, width), jnp.float32),
        ),
        in_specs=[smem, smem, smem, anyspace, anyspace, vmem],
        out_specs=(vmem, vmem),
        scratch_shapes=[
            pltpu.VMEM((block_count, tokens, width), jnp.bfloat16),
            pltpu.VMEM((block_count, tokens, width), jnp.bfloat16),
            pltpu.VMEM((block_count, tokens, width), jnp.float32),
            pltpu.VMEM((row_count, tokens, width), jnp.float32),
            pltpu.SemaphoreType.DMA((2, block_count)),
        ],
        cost_estimate=pl.CostEstimate(
            flops=6 * block_count * tokens * width * width,
            transcendentals=block_count * tokens * width,
            bytes_accessed=block_count * width * (4 * tokens + 6 * width)
            + row_count * tokens * width * 2,
        ),
    )(row_ids, col_ids, first, features, hidden_grad, weights)


def gather_over(x, axis):
    n = lax.axis_size(axis)
    return jnp.stack([x] + [shifted(x, axis, k) for k in range(1, n)])


def butterfly_gather(x, axis, bits):
    me = lax.axis_index(axis)
    held = x
    for bit in bits:
        other = swapped(held, axis, bit)
        mine_low = ((me >> bit) & 1) == 0
        held = jnp.where(mine_low, jnp.stack([held, other]), jnp.stack([other, held]))
    order = sorted(range(len(bits)), key=lambda a: -bits[len(bits) - 1 - a])
    perm = [order[i] for i in range(len(bits))] + list(range(len(bits), held.ndim))
    return jnp.transpose(held, perm)


def local(activations, out_grad, blocks, pattern, order):
    block_size = blocks.shape[-1]
    micro_count = activations.shape[1]
    tok_rows = activations.shape[1] * activations.shape[2]
    row_count = activations.shape[3] // block_size
    col_count = out_grad.shape[3] // block_size
    n_fsdp = lax.axis_size("fsdp")
    n_dp = lax.axis_size("dp")
    dp_bits = int(round(math.log2(n_dp)))
    assert 1 << dp_bits == n_dp and block_size % n_dp == 0
    chunk = block_size // n_dp
    me_dp = lax.axis_index("dp")

    own_blocks = blocks[0]
    blocks_dev = own_blocks.shape[0]

    assert n_fsdp % n_dp == 0
    per_dp = n_fsdp // n_dp
    weight_rows = blocks_dev * block_size
    assert 2 * blocks_dev <= block_size
    index_tile = jnp.zeros((16, block_size), jnp.bfloat16)
    index_tile = index_tile.at[0, : 2 * blocks_dev].set(
        pattern[0].reshape(-1).astype(jnp.bfloat16)
    )
    payload = jnp.concatenate([own_blocks.reshape(weight_rows, block_size), index_tile])
    fetched = []
    for m in range(per_dp):
        pairs = []
        for f in range(n_fsdp):
            for d in range(n_dp):
                k = d + n_dp * m
                pairs.append((((f - k) % n_fsdp) * n_dp + d, f * n_dp + d))
        fetched.append(lax.ppermute(payload, ("fsdp", "dp"), pairs))
    fetched = jnp.stack(fetched)
    pieces = butterfly_gather(fetched, "dp", list(reversed(range(dp_bits))))
    pieces = pieces.reshape((n_dp, per_dp) + payload.shape)
    pieces = jnp.transpose(pieces, (1, 0, 2, 3)).reshape((n_fsdp,) + payload.shape)
    weights = pieces[:, :weight_rows].reshape(n_fsdp * blocks_dev, block_size, block_size)
    all_indices = (
        pieces[:, weight_rows, : 2 * blocks_dev]
        .reshape(n_fsdp * blocks_dev, 2)
        .astype(jnp.int32)
    )

    row_ids = all_indices[:, 0]
    col_ids = all_indices[:, 1]
    input_grad, partial = block_pass(
        activations[0].reshape(tok_rows, -1),
        out_grad[0].reshape(tok_rows, -1),
        weights,
        row_ids,
        col_ids,
        row_count,
    )
    block_count = row_ids.shape[0]
    if block_count < row_count:
        hit = jnp.take(input_grad, row_ids, axis=0)
        payload = jnp.concatenate([hit.reshape(-1), row_ids.astype(jnp.bfloat16)])
        payload = passed_along(payload, "section", -1)
        got_rows = payload[hit.size:].astype(jnp.int32)
        got = payload[: hit.size].reshape(hit.shape)
        arrived = jnp.zeros_like(input_grad).at[got_rows].set(got)
    else:
        arrived = passed_along(input_grad, "section", -1)
    arrived = jnp.transpose(arrived, (1, 0, 2)).reshape(
        micro_count, activations.shape[2], activations.shape[3]
    )
    received = jnp.take(arrived, order, axis=0)

    held = partial.reshape((n_fsdp, blocks_dev) + (2,) * dp_bits + (chunk, block_size))
    for bit in range(dp_bits):
        axis_at = 2 + (dp_bits - 1 - bit)
        mine = (me_dp >> bit) & 1
        keep = lax.dynamic_index_in_dim(held, mine, axis_at, keepdims=False)
        send = lax.dynamic_index_in_dim(held, 1 - mine, axis_at, keepdims=False)
        if bit == 0:
            held = keep + swapped(send, "dp", bit)
        else:
            held = keep + swapped(send.astype(jnp.bfloat16), "dp", bit).astype(jnp.float32)
    me_fsdp = lax.axis_index("fsdp")
    to_device = (me_fsdp - jnp.arange(n_fsdp, dtype=jnp.int32)) % n_fsdp
    outgoing = jnp.take(held, to_device, axis=0).astype(jnp.bfloat16)
    incoming = lax.all_to_all(outgoing, "fsdp", 0, 0, tiled=True).astype(jnp.float32)
    others = jnp.arange(n_fsdp, dtype=jnp.int32) != me_fsdp
    incoming = jnp.where(others[:, None, None, None], incoming, 0.0)
    owned = held[0] + jnp.sum(incoming, axis=0)
    full = butterfly_gather(owned, "dp", list(reversed(range(dp_bits))))
    full = full.reshape((n_dp, blocks_dev, chunk, block_size))
    full = jnp.transpose(full, (1, 0, 2, 3)).reshape(blocks_dev, block_size, block_size)
    grad_scale = jnp.sqrt(jnp.float32(tok_rows * n_fsdp * n_dp))
    return (received[None], (full / grad_scale)[None])


def solution(mesh):
    in_specs = (
        P("section", None, ("fsdp", "dp"), None),
        P("section", None, ("fsdp", "dp"), None),
        P("section", "fsdp", None, None),
        P("section", "fsdp", None),
        P(),
    )
    out_specs = (P("section", None, ("fsdp", "dp"), None), P("section", "fsdp", None, None))
    return jax.shard_map(local, mesh=mesh, in_specs=in_specs, out_specs=out_specs, check_vma=False)
```

```python
import math

import jax
import jax.numpy as jnp
from jax import lax
from jax.experimental import pallas as pl
from jax.experimental.pallas import tpu as pltpu
from jax.sharding import PartitionSpec as P


def passed_along(block, axis, distance):
    devices = range(lax.axis_size(axis))
    route = [(i - distance, i) for i in devices if i - distance in devices]
    return lax.ppermute(block, axis, route)


def shifted(x, axis, k):
    n = lax.axis_size(axis)
    return lax.ppermute(x, axis, [(i, (i + k) % n) for i in range(n)])


def swapped(x, axis, bit):
    n = lax.axis_size(axis)
    return lax.ppermute(x, axis, [(i, i ^ (1 << bit)) for i in range(n)])


def silu_slope(pre_act):
    sigmoid_val = jax.nn.sigmoid(pre_act)
    return sigmoid_val * (1.0 + pre_act * (1.0 - sigmoid_val))


def block_kernel(rows_ref, cols_ref, rep_ref, feat_ref, hid_ref, w_ref, ig_ref, pg_ref,
                 xs, hs, pr, acc):
    block_count = w_ref.shape[0]
    width = w_ref.shape[-1]

    acc[...] = jnp.zeros(acc.shape, acc.dtype)

    @pl.loop(0, block_count)
    def _(b):
        r = pl.multiple_of(rows_ref[b] * width, width)
        c = pl.multiple_of(cols_ref[b] * width, width)
        xs[b] = feat_ref[:, pl.ds(r, width)]
        hs[b] = hid_ref[:, pl.ds(c, width)]
        pr[b] = jnp.dot(xs[b], w_ref[b], preferred_element_type=jnp.float32)

    @pl.loop(0, block_count)
    def _(b):
        first = rep_ref[b]

        @pl.when(first != b)
        def _():
            pr[first] = pr[first] + pr[b]

    @pl.loop(0, block_count)
    def _(b):
        pre_act = pr[rep_ref[b]]
        act = (hs[b].astype(jnp.float32) * silu_slope(pre_act)).astype(jnp.bfloat16)
        back = lax.dot_general(
            act, w_ref[b], (((1,), (1,)), ((), ())), preferred_element_type=jnp.float32
        )
        row = rows_ref[b]
        acc[row] = acc[row] + back
        pg_ref[b] = lax.dot_general(
            xs[b], act, (((0,), (0,)), ((), ())), preferred_element_type=jnp.float32
        )

    ig_ref[...] = acc[...].astype(ig_ref.dtype)


def block_pass(features, hidden_grad, weights, row_ids, col_ids, row_count):
    tokens = features.shape[0]
    block_count, width, _ = weights.shape
    same = col_ids[:, None] == col_ids[None, :]
    first = jnp.argmax(same, axis=1).astype(jnp.int32)
    smem = pl.BlockSpec(memory_space=pltpu.SMEM)
    vmem = pl.BlockSpec(memory_space=pltpu.VMEM)
    return pl.pallas_call(
        block_kernel,
        out_shape=(
            jax.ShapeDtypeStruct((row_count, tokens, width), jnp.bfloat16),
            jax.ShapeDtypeStruct((block_count, width, width), jnp.float32),
        ),
        in_specs=[smem, smem, smem, vmem, vmem, vmem],
        out_specs=(vmem, vmem),
        scratch_shapes=[
            pltpu.VMEM((block_count, tokens, width), jnp.bfloat16),
            pltpu.VMEM((block_count, tokens, width), jnp.bfloat16),
            pltpu.VMEM((block_count, tokens, width), jnp.float32),
            pltpu.VMEM((row_count, tokens, width), jnp.float32),
        ],
        cost_estimate=pl.CostEstimate(
            flops=6 * block_count * tokens * width * width,
            transcendentals=block_count * tokens * width,
            bytes_accessed=block_count * width * (4 * tokens + 6 * width)
            + row_count * tokens * width * 2,
        ),
    )(row_ids, col_ids, first, features, hidden_grad, weights)


def gather_over(x, axis):
    n = lax.axis_size(axis)
    return jnp.stack([x] + [shifted(x, axis, k) for k in range(1, n)])


def butterfly_gather(x, axis, bits):
    me = lax.axis_index(axis)
    held = x
    for bit in bits:
        other = swapped(held, axis, bit)
        mine_low = ((me >> bit) & 1) == 0
        held = jnp.where(mine_low, jnp.stack([held, other]), jnp.stack([other, held]))
    order = sorted(range(len(bits)), key=lambda a: -bits[len(bits) - 1 - a])
    perm = [order[i] for i in range(len(bits))] + list(range(len(bits), held.ndim))
    return jnp.transpose(held, perm)


def local(activations, out_grad, blocks, pattern, order):
    block_size = blocks.shape[-1]
    micro_count = activations.shape[1]
    tok_rows = activations.shape[1] * activations.shape[2]
    row_count = activations.shape[3] // block_size
    col_count = out_grad.shape[3] // block_size
    n_fsdp = lax.axis_size("fsdp")
    n_dp = lax.axis_size("dp")
    dp_bits = int(round(math.log2(n_dp)))
    assert 1 << dp_bits == n_dp and block_size % n_dp == 0
    chunk = block_size // n_dp
    me_dp = lax.axis_index("dp")

    own_blocks = blocks[0]
    blocks_dev = own_blocks.shape[0]

    assert n_fsdp % n_dp == 0
    per_dp = n_fsdp // n_dp
    weight_rows = blocks_dev * block_size
    assert 2 * blocks_dev <= block_size
    index_tile = jnp.zeros((16, block_size), jnp.bfloat16)
    index_tile = index_tile.at[0, : 2 * blocks_dev].set(
        pattern[0].reshape(-1).astype(jnp.bfloat16)
    )
    payload = jnp.concatenate([own_blocks.reshape(weight_rows, block_size), index_tile])
    fetched = []
    for m in range(per_dp):
        pairs = []
        for f in range(n_fsdp):
            for d in range(n_dp):
                k = d + n_dp * m
                pairs.append((((f - k) % n_fsdp) * n_dp + d, f * n_dp + d))
        fetched.append(lax.ppermute(payload, ("fsdp", "dp"), pairs))
    fetched = jnp.stack(fetched)
    pieces = butterfly_gather(fetched, "dp", list(reversed(range(dp_bits))))
    pieces = pieces.reshape((n_dp, per_dp) + payload.shape)
    pieces = jnp.transpose(pieces, (1, 0, 2, 3)).reshape((n_fsdp,) + payload.shape)
    weights = pieces[:, :weight_rows].reshape(n_fsdp * blocks_dev, block_size, block_size)
    all_indices = (
        pieces[:, weight_rows, : 2 * blocks_dev]
        .reshape(n_fsdp * blocks_dev, 2)
        .astype(jnp.int32)
    )

    row_ids = all_indices[:, 0]
    col_ids = all_indices[:, 1]
    input_grad, partial = block_pass(
        activations[0].reshape(tok_rows, -1),
        out_grad[0].reshape(tok_rows, -1),
        weights,
        row_ids,
        col_ids,
        row_count,
    )
    block_count = row_ids.shape[0]
    if block_count < row_count:
        hit = jnp.take(input_grad, row_ids, axis=0)
        payload = jnp.concatenate([hit.reshape(-1), row_ids.astype(jnp.bfloat16)])
        payload = passed_along(payload, "section", -1)
        got_rows = payload[hit.size:].astype(jnp.int32)
        got = payload[: hit.size].reshape(hit.shape)
        arrived = jnp.zeros_like(input_grad).at[got_rows].set(got)
    else:
        arrived = passed_along(input_grad, "section", -1)
    arrived = jnp.transpose(arrived, (1, 0, 2)).reshape(
        micro_count, activations.shape[2], activations.shape[3]
    )
    received = jnp.take(arrived, order, axis=0)

    held = partial.reshape((n_fsdp, blocks_dev) + (2,) * dp_bits + (chunk, block_size))
    for bit in range(dp_bits):
        axis_at = 2 + (dp_bits - 1 - bit)
        mine = (me_dp >> bit) & 1
        keep = lax.dynamic_index_in_dim(held, mine, axis_at, keepdims=False)
        send = lax.dynamic_index_in_dim(held, 1 - mine, axis_at, keepdims=False)
        if bit == 0:
            held = keep + swapped(send, "dp", bit)
        else:
            held = keep + swapped(send.astype(jnp.bfloat16), "dp", bit).astype(jnp.float32)
    owned = held[0]
    for k in range(1, n_fsdp):
        owned = owned + shifted(held[k].astype(jnp.bfloat16), "fsdp", -k).astype(jnp.float32)
    full = butterfly_gather(owned, "dp", list(reversed(range(dp_bits))))
    full = full.reshape((n_dp, blocks_dev, chunk, block_size))
    full = jnp.transpose(full, (1, 0, 2, 3)).reshape(blocks_dev, block_size, block_size)
    grad_scale = jnp.sqrt(jnp.float32(tok_rows * n_fsdp * n_dp))
    return (received[None], (full / grad_scale)[None])


def solution(mesh):
    in_specs = (
        P("section", None, ("fsdp", "dp"), None),
        P("section", None, ("fsdp", "dp"), None),
        P("section", "fsdp", None, None),
        P("section", "fsdp", None),
        P(),
    )
    out_specs = (P("section", None, ("fsdp", "dp"), None), P("section", "fsdp", None, None))
    return jax.shard_map(local, mesh=mesh, in_specs=in_specs, out_specs=out_specs, check_vma=False)
```

```python
import math

import jax
import jax.numpy as jnp
from jax import lax
from jax.experimental import pallas as pl
from jax.experimental.pallas import tpu as pltpu
from jax.sharding import PartitionSpec as P


def passed_along(block, axis, distance):
    devices = range(lax.axis_size(axis))
    route = [(i - distance, i) for i in devices if i - distance in devices]
    return lax.ppermute(block, axis, route)


def shifted(x, axis, k):
    n = lax.axis_size(axis)
    return lax.ppermute(x, axis, [(i, (i + k) % n) for i in range(n)])


def swapped(x, axis, bit):
    n = lax.axis_size(axis)
    return lax.ppermute(x, axis, [(i, i ^ (1 << bit)) for i in range(n)])


def silu_slope(pre_act):
    sigmoid_val = jax.nn.sigmoid(pre_act)
    return sigmoid_val * (1.0 + pre_act * (1.0 - sigmoid_val))


def block_kernel(rows_ref, cols_ref, rep_ref, feat_hbm, feat_t_hbm, hid_hbm, w_ref, ig_ref, pg_ref,
                 xs, xts, hs, pr, acc, sems):
    block_count = w_ref.shape[0]
    width = w_ref.shape[-1]

    def copies(b):
        r = pl.multiple_of(rows_ref[b] * width, width)
        c = pl.multiple_of(cols_ref[b] * width, width)
        return (
            pltpu.make_async_copy(feat_hbm.at[:, pl.ds(r, width)], xs.at[b], sems.at[0, b]),
            pltpu.make_async_copy(hid_hbm.at[:, pl.ds(c, width)], hs.at[b], sems.at[1, b]),
            pltpu.make_async_copy(feat_t_hbm.at[pl.ds(r, width), :], xts.at[b], sems.at[2, b]),
        )

    @pl.loop(0, block_count)
    def _(b):
        for cp in copies(b):
            cp.start()

    acc[...] = jnp.zeros(acc.shape, acc.dtype)

    @pl.loop(0, block_count)
    def _(b):
        for cp in copies(b):
            cp.wait()
        pr[b] = jnp.dot(xs[b], w_ref[b], preferred_element_type=jnp.float32)

    @pl.loop(0, block_count)
    def _(b):
        first = rep_ref[b]

        @pl.when(first != b)
        def _():
            pr[first] = pr[first] + pr[b]

    @pl.loop(0, block_count)
    def _(b):
        pre_act = pr[rep_ref[b]]
        act = (hs[b].astype(jnp.float32) * silu_slope(pre_act)).astype(jnp.bfloat16)
        back = lax.dot_general(
            act, w_ref[b], (((1,), (1,)), ((), ())), preferred_element_type=jnp.float32
        )
        row = rows_ref[b]
        acc[row] = acc[row] + back
        pg_ref[b] = jnp.dot(xts[b], act, preferred_element_type=jnp.float32)

    ig_ref[...] = acc[...].astype(ig_ref.dtype)


def block_pass(features, hidden_grad, weights, row_ids, col_ids, row_count):
    tokens = features.shape[0]
    block_count, width, _ = weights.shape
    same = col_ids[:, None] == col_ids[None, :]
    first = jnp.argmax(same, axis=1).astype(jnp.int32)
    smem = pl.BlockSpec(memory_space=pltpu.SMEM)
    anyspace = pl.BlockSpec(memory_space=pl.ANY)
    vmem = pl.BlockSpec(memory_space=pltpu.VMEM)
    return pl.pallas_call(
        block_kernel,
        out_shape=(
            jax.ShapeDtypeStruct((row_count, tokens, width), jnp.bfloat16),
            jax.ShapeDtypeStruct((block_count, width, width), jnp.float32),
        ),
        in_specs=[smem, smem, smem, anyspace, anyspace, anyspace, vmem],
        out_specs=(vmem, vmem),
        scratch_shapes=[
            pltpu.VMEM((block_count, tokens, width), jnp.bfloat16),
            pltpu.VMEM((block_count, width, tokens), jnp.bfloat16),
            pltpu.VMEM((block_count, tokens, width), jnp.bfloat16),
            pltpu.VMEM((block_count, tokens, width), jnp.float32),
            pltpu.VMEM((row_count, tokens, width), jnp.float32),
            pltpu.SemaphoreType.DMA((3, block_count)),
        ],
        cost_estimate=pl.CostEstimate(
            flops=6 * block_count * tokens * width * width,
            transcendentals=block_count * tokens * width,
            bytes_accessed=block_count * width * (4 * tokens + 6 * width)
            + row_count * tokens * width * 2,
        ),
    )(row_ids, col_ids, first, features, features.T, hidden_grad, weights)


def gather_over(x, axis):
    n = lax.axis_size(axis)
    return jnp.stack([x] + [shifted(x, axis, k) for k in range(1, n)])


def butterfly_gather(x, axis, bits):
    me = lax.axis_index(axis)
    held = x
    for bit in bits:
        other = swapped(held, axis, bit)
        mine_low = ((me >> bit) & 1) == 0
        held = jnp.where(mine_low, jnp.stack([held, other]), jnp.stack([other, held]))
    order = sorted(range(len(bits)), key=lambda a: -bits[len(bits) - 1 - a])
    perm = [order[i] for i in range(len(bits))] + list(range(len(bits), held.ndim))
    return jnp.transpose(held, perm)


def local(activations, out_grad, blocks, pattern, order):
    block_size = blocks.shape[-1]
    micro_count = activations.shape[1]
    tok_rows = activations.shape[1] * activations.shape[2]
    row_count = activations.shape[3] // block_size
    col_count = out_grad.shape[3] // block_size
    n_fsdp = lax.axis_size("fsdp")
    n_dp = lax.axis_size("dp")
    dp_bits = int(round(math.log2(n_dp)))
    assert 1 << dp_bits == n_dp and block_size % n_dp == 0
    chunk = block_size // n_dp
    me_dp = lax.axis_index("dp")

    own_blocks = blocks[0]
    blocks_dev = own_blocks.shape[0]

    assert n_fsdp % n_dp == 0
    per_dp = n_fsdp // n_dp
    weight_rows = blocks_dev * block_size
    assert 2 * blocks_dev <= block_size
    index_tile = jnp.zeros((16, block_size), jnp.bfloat16)
    index_tile = index_tile.at[0, : 2 * blocks_dev].set(
        pattern[0].reshape(-1).astype(jnp.bfloat16)
    )
    payload = jnp.concatenate([own_blocks.reshape(weight_rows, block_size), index_tile])
    fetched = []
    for m in range(per_dp):
        pairs = []
        for f in range(n_fsdp):
            for d in range(n_dp):
                k = d + n_dp * m
                pairs.append((((f - k) % n_fsdp) * n_dp + d, f * n_dp + d))
        fetched.append(lax.ppermute(payload, ("fsdp", "dp"), pairs))
    fetched = jnp.stack(fetched)
    pieces = butterfly_gather(fetched, "dp", list(reversed(range(dp_bits))))
    pieces = pieces.reshape((n_dp, per_dp) + payload.shape)
    pieces = jnp.transpose(pieces, (1, 0, 2, 3)).reshape((n_fsdp,) + payload.shape)
    weights = pieces[:, :weight_rows].reshape(n_fsdp * blocks_dev, block_size, block_size)
    all_indices = (
        pieces[:, weight_rows, : 2 * blocks_dev]
        .reshape(n_fsdp * blocks_dev, 2)
        .astype(jnp.int32)
    )

    row_ids = all_indices[:, 0]
    col_ids = all_indices[:, 1]
    input_grad, partial = block_pass(
        activations[0].reshape(tok_rows, -1),
        out_grad[0].reshape(tok_rows, -1),
        weights,
        row_ids,
        col_ids,
        row_count,
    )
    block_count = row_ids.shape[0]
    if block_count < row_count:
        hit = jnp.take(input_grad, row_ids, axis=0)
        payload = jnp.concatenate([hit.reshape(-1), row_ids.astype(jnp.bfloat16)])
        payload = passed_along(payload, "section", -1)
        got_rows = payload[hit.size:].astype(jnp.int32)
        got = payload[: hit.size].reshape(hit.shape)
        arrived = jnp.zeros_like(input_grad).at[got_rows].set(got)
    else:
        arrived = passed_along(input_grad, "section", -1)
    arrived = jnp.transpose(arrived, (1, 0, 2)).reshape(
        micro_count, activations.shape[2], activations.shape[3]
    )
    received = jnp.take(arrived, order, axis=0)

    held = partial.reshape((n_fsdp, blocks_dev) + (2,) * dp_bits + (chunk, block_size))
    for bit in range(dp_bits):
        axis_at = 2 + (dp_bits - 1 - bit)
        mine = (me_dp >> bit) & 1
        keep = lax.dynamic_index_in_dim(held, mine, axis_at, keepdims=False)
        send = lax.dynamic_index_in_dim(held, 1 - mine, axis_at, keepdims=False)
        if bit == 0:
            held = keep + swapped(send, "dp", bit)
        else:
            held = keep + swapped(send.astype(jnp.bfloat16), "dp", bit).astype(jnp.float32)
    owned = held[0]
    for k in range(1, n_fsdp):
        owned = owned + shifted(held[k].astype(jnp.bfloat16), "fsdp", -k).astype(jnp.float32)
    full = butterfly_gather(owned, "dp", list(reversed(range(dp_bits))))
    full = full.reshape((n_dp, blocks_dev, chunk, block_size))
    full = jnp.transpose(full, (1, 0, 2, 3)).reshape(blocks_dev, block_size, block_size)
    grad_scale = jnp.sqrt(jnp.float32(tok_rows * n_fsdp * n_dp))
    return (received[None], (full / grad_scale)[None])


def solution(mesh):
    in_specs = (
        P("section", None, ("fsdp", "dp"), None),
        P("section", None, ("fsdp", "dp"), None),
        P("section", "fsdp", None, None),
        P("section", "fsdp", None),
        P(),
    )
    out_specs = (P("section", None, ("fsdp", "dp"), None), P("section", "fsdp", None, None))
    return jax.shard_map(local, mesh=mesh, in_specs=in_specs, out_specs=out_specs, check_vma=False)
```

```python
import math

import jax
import jax.numpy as jnp
from jax import lax
from jax.experimental import pallas as pl
from jax.experimental.pallas import tpu as pltpu
from jax.sharding import PartitionSpec as P


def passed_along(block, axis, distance):
    devices = range(lax.axis_size(axis))
    route = [(i - distance, i) for i in devices if i - distance in devices]
    return lax.ppermute(block, axis, route)


def shifted(x, axis, k):
    n = lax.axis_size(axis)
    return lax.ppermute(x, axis, [(i, (i + k) % n) for i in range(n)])


def swapped(x, axis, bit):
    n = lax.axis_size(axis)
    return lax.ppermute(x, axis, [(i, i ^ (1 << bit)) for i in range(n)])


def silu_slope(pre_act):
    sigmoid_val = jax.nn.sigmoid(pre_act)
    return sigmoid_val * (1.0 + pre_act * (1.0 - sigmoid_val))


def block_kernel(rows_ref, cols_ref, rep_ref, feat_hbm, hid_hbm, w_ref, ig_ref, pg_ref,
                 xs, hs, pr, acc, sems):
    block_count = w_ref.shape[0]
    width = w_ref.shape[-1]

    def block_loop(body):
        def step(b, carry):
            body(b)
            return carry

        lax.fori_loop(0, block_count, step, 0, unroll=min(block_count, 16))

    def copies(b):
        r = pl.multiple_of(rows_ref[b] * width, width)
        c = pl.multiple_of(cols_ref[b] * width, width)
        return (
            pltpu.make_async_copy(feat_hbm.at[:, pl.ds(r, width)], xs.at[b], sems.at[0, b]),
            pltpu.make_async_copy(hid_hbm.at[:, pl.ds(c, width)], hs.at[b], sems.at[1, b]),
        )

    @block_loop
    def _(b):
        for cp in copies(b):
            cp.start()

    acc[...] = jnp.zeros(acc.shape, acc.dtype)

    @block_loop
    def _(b):
        for cp in copies(b):
            cp.wait()
        pr[b] = jnp.dot(xs[b], w_ref[b], preferred_element_type=jnp.float32)

    @block_loop
    def _(b):
        first = rep_ref[b]

        @pl.when(first != b)
        def _():
            pr[first] = pr[first] + pr[b]

    @block_loop
    def _(b):
        pre_act = pr[rep_ref[b]]
        act = (hs[b].astype(jnp.float32) * silu_slope(pre_act)).astype(jnp.bfloat16)
        back = lax.dot_general(
            act, w_ref[b], (((1,), (1,)), ((), ())), preferred_element_type=jnp.float32
        )
        row = rows_ref[b]
        acc[row] = acc[row] + back
        pg_ref[b] = lax.dot_general(
            xs[b], act, (((0,), (0,)), ((), ())), preferred_element_type=jnp.float32
        )

    ig_ref[...] = acc[...].astype(ig_ref.dtype)


def block_pass(features, hidden_grad, weights, row_ids, col_ids, row_count):
    tokens = features.shape[0]
    block_count, width, _ = weights.shape
    same = col_ids[:, None] == col_ids[None, :]
    first = jnp.argmax(same, axis=1).astype(jnp.int32)
    smem = pl.BlockSpec(memory_space=pltpu.SMEM)
    anyspace = pl.BlockSpec(memory_space=pl.ANY)
    vmem = pl.BlockSpec(memory_space=pltpu.VMEM)
    return pl.pallas_call(
        block_kernel,
        out_shape=(
            jax.ShapeDtypeStruct((row_count, tokens, width), jnp.bfloat16),
            jax.ShapeDtypeStruct((block_count, width, width), jnp.float32),
        ),
        in_specs=[smem, smem, smem, anyspace, anyspace, vmem],
        out_specs=(vmem, vmem),
        scratch_shapes=[
            pltpu.VMEM((block_count, tokens, width), jnp.bfloat16),
            pltpu.VMEM((block_count, tokens, width), jnp.bfloat16),
            pltpu.VMEM((block_count, tokens, width), jnp.float32),
            pltpu.VMEM((row_count, tokens, width), jnp.float32),
            pltpu.SemaphoreType.DMA((2, block_count)),
        ],
        cost_estimate=pl.CostEstimate(
            flops=6 * block_count * tokens * width * width,
            transcendentals=block_count * tokens * width,
            bytes_accessed=block_count * width * (4 * tokens + 6 * width)
            + row_count * tokens * width * 2,
        ),
    )(row_ids, col_ids, first, features, hidden_grad, weights)


def gather_over(x, axis):
    n = lax.axis_size(axis)
    return jnp.stack([x] + [shifted(x, axis, k) for k in range(1, n)])


def butterfly_gather(x, axis, bits):
    me = lax.axis_index(axis)
    held = x
    for bit in bits:
        other = swapped(held, axis, bit)
        mine_low = ((me >> bit) & 1) == 0
        held = jnp.where(mine_low, jnp.stack([held, other]), jnp.stack([other, held]))
    order = sorted(range(len(bits)), key=lambda a: -bits[len(bits) - 1 - a])
    perm = [order[i] for i in range(len(bits))] + list(range(len(bits), held.ndim))
    return jnp.transpose(held, perm)


def local(activations, out_grad, blocks, pattern, order):
    block_size = blocks.shape[-1]
    micro_count = activations.shape[1]
    tok_rows = activations.shape[1] * activations.shape[2]
    row_count = activations.shape[3] // block_size
    col_count = out_grad.shape[3] // block_size
    n_fsdp = lax.axis_size("fsdp")
    n_dp = lax.axis_size("dp")
    dp_bits = int(round(math.log2(n_dp)))
    assert 1 << dp_bits == n_dp and block_size % n_dp == 0
    chunk = block_size // n_dp
    me_dp = lax.axis_index("dp")

    own_blocks = blocks[0]
    blocks_dev = own_blocks.shape[0]

    assert n_fsdp % n_dp == 0
    per_dp = n_fsdp // n_dp
    weight_rows = blocks_dev * block_size
    assert 2 * blocks_dev <= block_size
    index_tile = jnp.zeros((16, block_size), jnp.bfloat16)
    index_tile = index_tile.at[0, : 2 * blocks_dev].set(
        pattern[0].reshape(-1).astype(jnp.bfloat16)
    )
    payload = jnp.concatenate([own_blocks.reshape(weight_rows, block_size), index_tile])
    fetched = []
    for m in range(per_dp):
        pairs = []
        for f in range(n_fsdp):
            for d in range(n_dp):
                k = d + n_dp * m
                pairs.append((((f - k) % n_fsdp) * n_dp + d, f * n_dp + d))
        fetched.append(lax.ppermute(payload, ("fsdp", "dp"), pairs))
    fetched = jnp.stack(fetched)
    pieces = butterfly_gather(fetched, "dp", list(reversed(range(dp_bits))))
    pieces = pieces.reshape((n_dp, per_dp) + payload.shape)
    pieces = jnp.transpose(pieces, (1, 0, 2, 3)).reshape((n_fsdp,) + payload.shape)
    weights = pieces[:, :weight_rows].reshape(n_fsdp * blocks_dev, block_size, block_size)
    all_indices = (
        pieces[:, weight_rows, : 2 * blocks_dev]
        .reshape(n_fsdp * blocks_dev, 2)
        .astype(jnp.int32)
    )

    row_ids = all_indices[:, 0]
    col_ids = all_indices[:, 1]
    input_grad, partial = block_pass(
        activations[0].reshape(tok_rows, -1),
        out_grad[0].reshape(tok_rows, -1),
        weights,
        row_ids,
        col_ids,
        row_count,
    )
    block_count = row_ids.shape[0]
    if block_count < row_count:
        hit = jnp.take(input_grad, row_ids, axis=0)
        payload = jnp.concatenate([hit.reshape(-1), row_ids.astype(jnp.bfloat16)])
        payload = passed_along(payload, "section", -1)
        got_rows = payload[hit.size:].astype(jnp.int32)
        got = payload[: hit.size].reshape(hit.shape)
        arrived = jnp.zeros_like(input_grad).at[got_rows].set(got)
    else:
        arrived = passed_along(input_grad, "section", -1)
    arrived = jnp.transpose(arrived, (1, 0, 2)).reshape(
        micro_count, activations.shape[2], activations.shape[3]
    )
    received = jnp.take(arrived, order, axis=0)

    held = partial.reshape((n_fsdp, blocks_dev) + (2,) * dp_bits + (chunk, block_size))
    for bit in range(dp_bits):
        axis_at = 2 + (dp_bits - 1 - bit)
        mine = (me_dp >> bit) & 1
        keep = lax.dynamic_index_in_dim(held, mine, axis_at, keepdims=False)
        send = lax.dynamic_index_in_dim(held, 1 - mine, axis_at, keepdims=False)
        if bit == 0:
            held = keep + swapped(send, "dp", bit)
        else:
            held = keep + swapped(send.astype(jnp.bfloat16), "dp", bit).astype(jnp.float32)
    owned = held[0]
    for k in range(1, n_fsdp):
        owned = owned + shifted(held[k].astype(jnp.bfloat16), "fsdp", -k).astype(jnp.float32)
    full = butterfly_gather(owned, "dp", list(reversed(range(dp_bits))))
    full = full.reshape((n_dp, blocks_dev, chunk, block_size))
    full = jnp.transpose(full, (1, 0, 2, 3)).reshape(blocks_dev, block_size, block_size)
    grad_scale = jnp.sqrt(jnp.float32(tok_rows * n_fsdp * n_dp))
    return (received[None], (full / grad_scale)[None])


def solution(mesh):
    in_specs = (
        P("section", None, ("fsdp", "dp"), None),
        P("section", None, ("fsdp", "dp"), None),
        P("section", "fsdp", None, None),
        P("section", "fsdp", None),
        P(),
    )
    out_specs = (P("section", None, ("fsdp", "dp"), None), P("section", "fsdp", None, None))
    return jax.shard_map(local, mesh=mesh, in_specs=in_specs, out_specs=out_specs, check_vma=False)
```

```python
import functools
import math

import jax
import jax.numpy as jnp
from jax import lax
from jax.experimental import pallas as pl
from jax.experimental.pallas import tpu as pltpu
from jax.sharding import PartitionSpec as P


def passed_along(block, axis, distance):
    devices = range(lax.axis_size(axis))
    route = [(i - distance, i) for i in devices if i - distance in devices]
    return lax.ppermute(block, axis, route)


def shifted(x, axis, k):
    n = lax.axis_size(axis)
    return lax.ppermute(x, axis, [(i, (i + k) % n) for i in range(n)])


def swapped(x, axis, bit):
    n = lax.axis_size(axis)
    return lax.ppermute(x, axis, [(i, i ^ (1 << bit)) for i in range(n)])


def silu_slope(pre_act):
    sigmoid_val = jax.nn.sigmoid(pre_act)
    return sigmoid_val * (1.0 + pre_act * (1.0 - sigmoid_val))


def block_kernel(compact, chunk, rows_ref, cols_ref, rep_ref, bit_ref, feat_hbm, hid_hbm, w_ref,
                 ig_ref, keep_ref, send_ref, xs, hs, pr, acc, pgs, sems):
    block_count = w_ref.shape[0]
    width = w_ref.shape[-1]
    halves = keep_ref.shape[1]

    def block_loop(body):
        def step(b, carry):
            body(b)
            return carry

        lax.fori_loop(0, block_count, step, 0, unroll=min(block_count, 16))

    def copies(b):
        r = pl.multiple_of(rows_ref[b] * width, width)
        c = pl.multiple_of(cols_ref[b] * width, width)
        return (
            pltpu.make_async_copy(feat_hbm.at[:, pl.ds(r, width)], xs.at[b], sems.at[0, b]),
            pltpu.make_async_copy(hid_hbm.at[:, pl.ds(c, width)], hs.at[b], sems.at[1, b]),
        )

    @block_loop
    def _(b):
        for cp in copies(b):
            cp.start()

    if compact:
        @block_loop
        def _(b):
            acc[rows_ref[b]] = jnp.zeros(acc.shape[1:], acc.dtype)
    else:
        acc[...] = jnp.zeros(acc.shape, acc.dtype)

    @block_loop
    def _(b):
        for cp in copies(b):
            cp.wait()
        pr[b] = jnp.dot(xs[b], w_ref[b], preferred_element_type=jnp.float32)

    @block_loop
    def _(b):
        first = rep_ref[b]

        @pl.when(first != b)
        def _():
            pr[first] = pr[first] + pr[b]

    mine = bit_ref[0]

    @block_loop
    def _(b):
        pre_act = pr[rep_ref[b]]
        act = (hs[b].astype(jnp.float32) * silu_slope(pre_act)).astype(jnp.bfloat16)
        back = lax.dot_general(
            act, w_ref[b], (((1,), (1,)), ((), ())), preferred_element_type=jnp.float32
        )
        row = rows_ref[b]
        acc[row] = acc[row] + back
        pgs[b] = lax.dot_general(
            xs[b], act, (((0,), (0,)), ((), ())), preferred_element_type=jnp.float32
        )
        for h in range(halves):
            kept = pl.multiple_of((2 * h + mine) * chunk, chunk)
            sent = pl.multiple_of((2 * h + 1 - mine) * chunk, chunk)
            keep_ref[b, h] = pgs[b, pl.ds(kept, chunk), :]
            send_ref[b, h] = pgs[b, pl.ds(sent, chunk), :]

    if compact:
        @block_loop
        def _(b):
            ig_ref[b] = acc[rows_ref[b]].astype(ig_ref.dtype)
    else:
        ig_ref[...] = acc[...].astype(ig_ref.dtype)


def block_pass(features, hidden_grad, weights, row_ids, col_ids, row_count, low_bit, parts):
    tokens = features.shape[0]
    block_count, width, _ = weights.shape
    chunk = width // parts
    compact = block_count < row_count
    same = col_ids[:, None] == col_ids[None, :]
    first = jnp.argmax(same, axis=1).astype(jnp.int32)
    smem = pl.BlockSpec(memory_space=pltpu.SMEM)
    anyspace = pl.BlockSpec(memory_space=pl.ANY)
    vmem = pl.BlockSpec(memory_space=pltpu.VMEM)
    ig_rows = block_count if compact else row_count
    half = jax.ShapeDtypeStruct((block_count, parts // 2, chunk, width), jnp.float32)
    return pl.pallas_call(
        functools.partial(block_kernel, compact, chunk),
        out_shape=(
            jax.ShapeDtypeStruct((ig_rows, tokens, width), jnp.bfloat16),
            half,
            half,
        ),
        in_specs=[smem, smem, smem, smem, anyspace, anyspace, vmem],
        out_specs=(vmem, vmem, vmem),
        scratch_shapes=[
            pltpu.VMEM((block_count, tokens, width), jnp.bfloat16),
            pltpu.VMEM((block_count, tokens, width), jnp.bfloat16),
            pltpu.VMEM((block_count, tokens, width), jnp.float32),
            pltpu.VMEM((row_count, tokens, width), jnp.float32),
            pltpu.VMEM((block_count, width, width), jnp.float32),
            pltpu.SemaphoreType.DMA((2, block_count)),
        ],
        cost_estimate=pl.CostEstimate(
            flops=6 * block_count * tokens * width * width,
            transcendentals=block_count * tokens * width,
            bytes_accessed=block_count * width * (4 * tokens + 6 * width)
            + row_count * tokens * width * 2,
        ),
    )(row_ids, col_ids, first, low_bit, features, hidden_grad, weights)


def gather_over(x, axis):
    n = lax.axis_size(axis)
    return jnp.stack([x] + [shifted(x, axis, k) for k in range(1, n)])


def butterfly_gather(x, axis, bits):
    me = lax.axis_index(axis)
    held = x
    for bit in bits:
        other = swapped(held, axis, bit)
        mine_low = ((me >> bit) & 1) == 0
        held = jnp.where(mine_low, jnp.stack([held, other]), jnp.stack([other, held]))
    order = sorted(range(len(bits)), key=lambda a: -bits[len(bits) - 1 - a])
    perm = [order[i] for i in range(len(bits))] + list(range(len(bits), held.ndim))
    return jnp.transpose(held, perm)


def local(activations, out_grad, blocks, pattern, order):
    block_size = blocks.shape[-1]
    micro_count = activations.shape[1]
    tok_rows = activations.shape[1] * activations.shape[2]
    row_count = activations.shape[3] // block_size
    col_count = out_grad.shape[3] // block_size
    n_fsdp = lax.axis_size("fsdp")
    n_dp = lax.axis_size("dp")
    dp_bits = int(round(math.log2(n_dp)))
    assert 1 << dp_bits == n_dp and block_size % n_dp == 0
    chunk = block_size // n_dp
    me_dp = lax.axis_index("dp")

    own_blocks = blocks[0]
    blocks_dev = own_blocks.shape[0]

    assert n_fsdp % n_dp == 0
    per_dp = n_fsdp // n_dp
    weight_rows = blocks_dev * block_size
    assert 2 * blocks_dev <= block_size
    index_tile = jnp.zeros((16, block_size), jnp.bfloat16)
    index_tile = index_tile.at[0, : 2 * blocks_dev].set(
        pattern[0].reshape(-1).astype(jnp.bfloat16)
    )
    payload = jnp.concatenate([own_blocks.reshape(weight_rows, block_size), index_tile])
    fetched = []
    for m in range(per_dp):
        pairs = []
        for f in range(n_fsdp):
            for d in range(n_dp):
                k = d + n_dp * m
                pairs.append((((f - k) % n_fsdp) * n_dp + d, f * n_dp + d))
        fetched.append(lax.ppermute(payload, ("fsdp", "dp"), pairs))
    fetched = jnp.stack(fetched)
    pieces = butterfly_gather(fetched, "dp", list(reversed(range(dp_bits))))
    pieces = pieces.reshape((n_dp, per_dp) + payload.shape)
    pieces = jnp.transpose(pieces, (1, 0, 2, 3)).reshape((n_fsdp,) + payload.shape)
    weights = pieces[:, :weight_rows].reshape(n_fsdp * blocks_dev, block_size, block_size)
    all_indices = (
        pieces[:, weight_rows, : 2 * blocks_dev]
        .reshape(n_fsdp * blocks_dev, 2)
        .astype(jnp.int32)
    )

    row_ids = all_indices[:, 0]
    col_ids = all_indices[:, 1]
    low_bit = (me_dp & 1).astype(jnp.int32).reshape(1)
    input_grad, keep, send = block_pass(
        activations[0].reshape(tok_rows, -1),
        out_grad[0].reshape(tok_rows, -1),
        weights,
        row_ids,
        col_ids,
        row_count,
        low_bit,
        n_dp,
    )
    block_count = row_ids.shape[0]
    if block_count < row_count:
        payload = jnp.concatenate([input_grad.reshape(-1), row_ids.astype(jnp.bfloat16)])
        payload = passed_along(payload, "section", -1)
        got_rows = payload[input_grad.size :].astype(jnp.int32)
        got = payload[: input_grad.size].reshape(input_grad.shape)
        arrived = jnp.zeros((row_count,) + input_grad.shape[1:], jnp.bfloat16)
        arrived = arrived.at[got_rows].set(got)
    else:
        arrived = passed_along(input_grad, "section", -1)
    arrived = jnp.transpose(arrived, (1, 0, 2)).reshape(
        micro_count, activations.shape[2], activations.shape[3]
    )
    received = jnp.take(arrived, order, axis=0)

    held = keep + swapped(send, "dp", 0)
    held = held.reshape((n_fsdp, blocks_dev) + (2,) * (dp_bits - 1) + (chunk, block_size))
    for bit in range(1, dp_bits):
        axis_at = 2 + (dp_bits - 1 - bit)
        mine = (me_dp >> bit) & 1
        keep = lax.dynamic_index_in_dim(held, mine, axis_at, keepdims=False)
        send = lax.dynamic_index_in_dim(held, 1 - mine, axis_at, keepdims=False)
        held = keep + swapped(send.astype(jnp.bfloat16), "dp", bit).astype(jnp.float32)
    owned = held[0]
    for k in range(1, n_fsdp):
        owned = owned + shifted(held[k].astype(jnp.bfloat16), "fsdp", -k).astype(jnp.float32)
    full = butterfly_gather(owned, "dp", list(reversed(range(dp_bits))))
    full = full.reshape((n_dp, blocks_dev, chunk, block_size))
    full = jnp.transpose(full, (1, 0, 2, 3)).reshape(blocks_dev, block_size, block_size)
    grad_scale = jnp.sqrt(jnp.float32(tok_rows * n_fsdp * n_dp))
    return (received[None], (full / grad_scale)[None])


def solution(mesh):
    in_specs = (
        P("section", None, ("fsdp", "dp"), None),
        P("section", None, ("fsdp", "dp"), None),
        P("section", "fsdp", None, None),
        P("section", "fsdp", None),
        P(),
    )
    out_specs = (P("section", None, ("fsdp", "dp"), None), P("section", "fsdp", None, None))
    return jax.shard_map(local, mesh=mesh, in_specs=in_specs, out_specs=out_specs, check_vma=False)
```

```python
import functools
import math

import jax
import jax.numpy as jnp
from jax import lax
from jax.experimental import pallas as pl
from jax.experimental.pallas import tpu as pltpu
from jax.sharding import PartitionSpec as P


def passed_along(block, axis, distance):
    devices = range(lax.axis_size(axis))
    route = [(i - distance, i) for i in devices if i - distance in devices]
    return lax.ppermute(block, axis, route)


def shifted(x, axis, k):
    n = lax.axis_size(axis)
    return lax.ppermute(x, axis, [(i, (i + k) % n) for i in range(n)])


def swapped(x, axis, bit):
    n = lax.axis_size(axis)
    return lax.ppermute(x, axis, [(i, i ^ (1 << bit)) for i in range(n)])


def silu_slope(pre_act):
    sigmoid_val = jax.nn.sigmoid(pre_act)
    return sigmoid_val * (1.0 + pre_act * (1.0 - sigmoid_val))


def block_kernel(compact, chunk, rows_ref, cols_ref, rep_ref, bit_ref, feat_hbm, hid_hbm, w_ref,
                 ig_ref, keep_ref, send_ref, xs, hs, pr, acc, pgs, sems):
    block_count = w_ref.shape[0]
    width = w_ref.shape[-1]
    halves = keep_ref.shape[1]

    def block_loop(body):
        def step(b, carry):
            body(b)
            return carry

        lax.fori_loop(0, block_count, step, 0, unroll=min(block_count, 16))

    def copies(b):
        r = pl.multiple_of(rows_ref[b] * width, width)
        c = pl.multiple_of(cols_ref[b] * width, width)
        return (
            pltpu.make_async_copy(feat_hbm.at[:, pl.ds(r, width)], xs.at[b], sems.at[0, b]),
            pltpu.make_async_copy(hid_hbm.at[:, pl.ds(c, width)], hs.at[b], sems.at[1, b]),
        )

    @block_loop
    def _(b):
        for cp in copies(b):
            cp.start()

    if compact:
        @block_loop
        def _(b):
            acc[rows_ref[b]] = jnp.zeros(acc.shape[1:], acc.dtype)
    else:
        acc[...] = jnp.zeros(acc.shape, acc.dtype)

    @block_loop
    def _(b):
        for cp in copies(b):
            cp.wait()
        pr[b] = jnp.dot(xs[b], w_ref[b], preferred_element_type=jnp.float32)

    @block_loop
    def _(b):
        first = rep_ref[b]

        @pl.when(first != b)
        def _():
            pr[first] = pr[first] + pr[b]

    mine = bit_ref[0]

    @block_loop
    def _(b):
        pre_act = pr[rep_ref[b]]
        act = (hs[b].astype(jnp.float32) * silu_slope(pre_act)).astype(jnp.bfloat16)
        back = lax.dot_general(
            act, w_ref[b], (((1,), (1,)), ((), ())), preferred_element_type=jnp.float32
        )
        row = rows_ref[b]
        acc[row] = acc[row] + back
        pgs[b] = lax.dot_general(
            xs[b], act, (((0,), (0,)), ((), ())), preferred_element_type=jnp.float32
        )
        for h in range(halves):
            kept = pl.multiple_of((2 * h + mine) * chunk, chunk)
            sent = pl.multiple_of((2 * h + 1 - mine) * chunk, chunk)
            keep_ref[b, h] = pgs[b, pl.ds(kept, chunk), :]
            send_ref[b, h] = pgs[b, pl.ds(sent, chunk), :]

    if compact:
        @block_loop
        def _(b):
            ig_ref[b] = acc[rows_ref[b]].astype(ig_ref.dtype)
    else:
        ig_ref[...] = acc[...].astype(ig_ref.dtype)


def block_pass(features, hidden_grad, weights, row_ids, col_ids, row_count, low_bit, parts):
    tokens = features.shape[0]
    block_count, width, _ = weights.shape
    chunk = width // parts
    compact = block_count < row_count
    same = col_ids[:, None] == col_ids[None, :]
    first = jnp.argmax(same, axis=1).astype(jnp.int32)
    smem = pl.BlockSpec(memory_space=pltpu.SMEM)
    anyspace = pl.BlockSpec(memory_space=pl.ANY)
    vmem = pl.BlockSpec(memory_space=pltpu.VMEM)
    ig_rows = block_count if compact else row_count
    half = jax.ShapeDtypeStruct((block_count, parts // 2, chunk, width), jnp.float32)
    return pl.pallas_call(
        functools.partial(block_kernel, compact, chunk),
        out_shape=(
            jax.ShapeDtypeStruct((ig_rows, tokens, width), jnp.bfloat16),
            half,
            half,
        ),
        in_specs=[smem, smem, smem, smem, anyspace, anyspace, vmem],
        out_specs=(vmem, vmem, vmem),
        scratch_shapes=[
            pltpu.VMEM((block_count, tokens, width), jnp.bfloat16),
            pltpu.VMEM((block_count, tokens, width), jnp.bfloat16),
            pltpu.VMEM((block_count, tokens, width), jnp.float32),
            pltpu.VMEM((row_count, tokens, width), jnp.float32),
            pltpu.VMEM((block_count, width, width), jnp.float32),
            pltpu.SemaphoreType.DMA((2, block_count)),
        ],
        cost_estimate=pl.CostEstimate(
            flops=6 * block_count * tokens * width * width,
            transcendentals=block_count * tokens * width,
            bytes_accessed=block_count * width * (4 * tokens + 6 * width)
            + row_count * tokens * width * 2,
        ),
    )(row_ids, col_ids, first, low_bit, features, hidden_grad, weights)


def unpack_kernel(rows_ref, order_ref, got_ref, out_ref, where_ref):
    block_count, tok_rows, width = got_ref.shape
    micro_count, tok_mb, _ = out_ref.shape
    row_count = out_ref.shape[2] // width
    for r in range(row_count):
        where_ref[r] = -1
    for b in range(block_count):
        where_ref[rows_ref[b]] = b
    for r in range(row_count):
        src = where_ref[r]
        for i in range(micro_count):
            start = pl.multiple_of(order_ref[i] * tok_mb, tok_mb)

            @pl.when(src >= 0)
            def _():
                out_ref[i, :, r * width : (r + 1) * width] = got_ref[
                    src, pl.ds(start, tok_mb), :
                ]

            @pl.when(src < 0)
            def _():
                out_ref[i, :, r * width : (r + 1) * width] = jnp.zeros(
                    (tok_mb, width), out_ref.dtype
                )


def unpack_rows(got_rows, order, got, micro_count, row_count):
    block_count, tok_rows, width = got.shape
    smem = pl.BlockSpec(memory_space=pltpu.SMEM)
    vmem = pl.BlockSpec(memory_space=pltpu.VMEM)
    return pl.pallas_call(
        unpack_kernel,
        out_shape=jax.ShapeDtypeStruct(
            (micro_count, tok_rows // micro_count, row_count * width), got.dtype
        ),
        in_specs=[smem, smem, vmem],
        out_specs=vmem,
        scratch_shapes=[pltpu.SMEM((row_count,), jnp.int32)],
    )(got_rows, order, got)


def gather_over(x, axis):
    n = lax.axis_size(axis)
    return jnp.stack([x] + [shifted(x, axis, k) for k in range(1, n)])


def butterfly_gather(x, axis, bits):
    me = lax.axis_index(axis)
    held = x
    for bit in bits:
        other = swapped(held, axis, bit)
        mine_low = ((me >> bit) & 1) == 0
        held = jnp.where(mine_low, jnp.stack([held, other]), jnp.stack([other, held]))
    order = sorted(range(len(bits)), key=lambda a: -bits[len(bits) - 1 - a])
    perm = [order[i] for i in range(len(bits))] + list(range(len(bits), held.ndim))
    return jnp.transpose(held, perm)


def local(activations, out_grad, blocks, pattern, order):
    block_size = blocks.shape[-1]
    micro_count = activations.shape[1]
    tok_rows = activations.shape[1] * activations.shape[2]
    row_count = activations.shape[3] // block_size
    col_count = out_grad.shape[3] // block_size
    n_fsdp = lax.axis_size("fsdp")
    n_dp = lax.axis_size("dp")
    dp_bits = int(round(math.log2(n_dp)))
    assert 1 << dp_bits == n_dp and block_size % n_dp == 0
    chunk = block_size // n_dp
    me_dp = lax.axis_index("dp")

    own_blocks = blocks[0]
    blocks_dev = own_blocks.shape[0]

    assert n_fsdp % n_dp == 0
    per_dp = n_fsdp // n_dp
    weight_rows = blocks_dev * block_size
    assert 2 * blocks_dev <= block_size
    index_tile = jnp.zeros((16, block_size), jnp.bfloat16)
    index_tile = index_tile.at[0, : 2 * blocks_dev].set(
        pattern[0].reshape(-1).astype(jnp.bfloat16)
    )
    payload = jnp.concatenate([own_blocks.reshape(weight_rows, block_size), index_tile])
    fetched = []
    for m in range(per_dp):
        pairs = []
        for f in range(n_fsdp):
            for d in range(n_dp):
                k = d + n_dp * m
                pairs.append((((f - k) % n_fsdp) * n_dp + d, f * n_dp + d))
        fetched.append(lax.ppermute(payload, ("fsdp", "dp"), pairs))
    fetched = jnp.stack(fetched)
    pieces = butterfly_gather(fetched, "dp", list(reversed(range(dp_bits))))
    pieces = pieces.reshape((n_dp, per_dp) + payload.shape)
    pieces = jnp.transpose(pieces, (1, 0, 2, 3)).reshape((n_fsdp,) + payload.shape)
    weights = pieces[:, :weight_rows].reshape(n_fsdp * blocks_dev, block_size, block_size)
    all_indices = (
        pieces[:, weight_rows, : 2 * blocks_dev]
        .reshape(n_fsdp * blocks_dev, 2)
        .astype(jnp.int32)
    )

    row_ids = all_indices[:, 0]
    col_ids = all_indices[:, 1]
    low_bit = (me_dp & 1).astype(jnp.int32).reshape(1)
    input_grad, keep, send = block_pass(
        activations[0].reshape(tok_rows, -1),
        out_grad[0].reshape(tok_rows, -1),
        weights,
        row_ids,
        col_ids,
        row_count,
        low_bit,
        n_dp,
    )
    block_count = row_ids.shape[0]
    if block_count < row_count:
        payload = jnp.concatenate([input_grad.reshape(-1), row_ids.astype(jnp.bfloat16)])
        payload = passed_along(payload, "section", -1)
        got_rows = payload[input_grad.size :].astype(jnp.int32)
        got = payload[: input_grad.size].reshape(input_grad.shape)
        received = unpack_rows(got_rows, order, got, micro_count, row_count)
    else:
        arrived = passed_along(input_grad, "section", -1)
        arrived = jnp.transpose(arrived, (1, 0, 2)).reshape(
            micro_count, activations.shape[2], activations.shape[3]
        )
        received = jnp.take(arrived, order, axis=0)

    held = keep + swapped(send, "dp", 0)
    held = held.reshape((n_fsdp, blocks_dev) + (2,) * (dp_bits - 1) + (chunk, block_size))
    for bit in range(1, dp_bits):
        axis_at = 2 + (dp_bits - 1 - bit)
        mine = (me_dp >> bit) & 1
        keep = lax.dynamic_index_in_dim(held, mine, axis_at, keepdims=False)
        send = lax.dynamic_index_in_dim(held, 1 - mine, axis_at, keepdims=False)
        held = keep + swapped(send.astype(jnp.bfloat16), "dp", bit).astype(jnp.float32)
    owned = held[0]
    for k in range(1, n_fsdp):
        owned = owned + shifted(held[k].astype(jnp.bfloat16), "fsdp", -k).astype(jnp.float32)
    full = butterfly_gather(owned, "dp", list(reversed(range(dp_bits))))
    full = full.reshape((n_dp, blocks_dev, chunk, block_size))
    full = jnp.transpose(full, (1, 0, 2, 3)).reshape(blocks_dev, block_size, block_size)
    grad_scale = jnp.sqrt(jnp.float32(tok_rows * n_fsdp * n_dp))
    return (received[None], (full / grad_scale)[None])


def solution(mesh):
    in_specs = (
        P("section", None, ("fsdp", "dp"), None),
        P("section", None, ("fsdp", "dp"), None),
        P("section", "fsdp", None, None),
        P("section", "fsdp", None),
        P(),
    )
    out_specs = (P("section", None, ("fsdp", "dp"), None), P("section", "fsdp", None, None))
    return jax.shard_map(local, mesh=mesh, in_specs=in_specs, out_specs=out_specs, check_vma=False)
```

```python
import functools
import math

import jax
import jax.numpy as jnp
from jax import lax
from jax.experimental import pallas as pl
from jax.experimental.pallas import tpu as pltpu
from jax.sharding import PartitionSpec as P


def passed_along(block, axis, distance):
    devices = range(lax.axis_size(axis))
    route = [(i - distance, i) for i in devices if i - distance in devices]
    return lax.ppermute(block, axis, route)


def shifted(x, axis, k):
    n = lax.axis_size(axis)
    return lax.ppermute(x, axis, [(i, (i + k) % n) for i in range(n)])


def swapped(x, axis, bit):
    n = lax.axis_size(axis)
    return lax.ppermute(x, axis, [(i, i ^ (1 << bit)) for i in range(n)])


def silu_slope(pre_act):
    sigmoid_val = jax.nn.sigmoid(pre_act)
    return sigmoid_val * (1.0 + pre_act * (1.0 - sigmoid_val))


def block_kernel(compact, chunk, rows_ref, cols_ref, rep_ref, bit_ref, feat_hbm, hid_hbm, w_ref,
                 ig_ref, keep_ref, send_ref, xs, hs, pr, acc, pgs, sems):
    block_count = w_ref.shape[0]
    width = w_ref.shape[-1]
    halves = keep_ref.shape[1]

    def block_loop(body):
        def step(b, carry):
            body(b)
            return carry

        lax.fori_loop(0, block_count, step, 0, unroll=min(block_count, 16))

    def copies(b):
        r = pl.multiple_of(rows_ref[b] * width, width)
        c = pl.multiple_of(cols_ref[b] * width, width)
        return (
            pltpu.make_async_copy(feat_hbm.at[:, pl.ds(r, width)], xs.at[b], sems.at[0, b]),
            pltpu.make_async_copy(hid_hbm.at[:, pl.ds(c, width)], hs.at[b], sems.at[1, b]),
        )

    @block_loop
    def _(b):
        for cp in copies(b):
            cp.start()

    if compact:
        @block_loop
        def _(b):
            acc[rows_ref[b]] = jnp.zeros(acc.shape[1:], acc.dtype)
    else:
        acc[...] = jnp.zeros(acc.shape, acc.dtype)

    @block_loop
    def _(b):
        for cp in copies(b):
            cp.wait()
        pr[b] = jnp.dot(xs[b], w_ref[b], preferred_element_type=jnp.float32)

    @block_loop
    def _(b):
        first = rep_ref[b]

        @pl.when(first != b)
        def _():
            pr[first] = pr[first] + pr[b]

    mine = bit_ref[0]

    @block_loop
    def _(b):
        pre_act = pr[rep_ref[b]]
        act = (hs[b].astype(jnp.float32) * silu_slope(pre_act)).astype(jnp.bfloat16)
        back = lax.dot_general(
            act, w_ref[b], (((1,), (1,)), ((), ())), preferred_element_type=jnp.float32
        )
        row = rows_ref[b]
        acc[row] = acc[row] + back
        pgs[b] = lax.dot_general(
            xs[b], act, (((0,), (0,)), ((), ())), preferred_element_type=jnp.float32
        )
        for h in range(halves):
            kept = pl.multiple_of((2 * h + mine) * chunk, chunk)
            sent = pl.multiple_of((2 * h + 1 - mine) * chunk, chunk)
            keep_ref[b, h] = pgs[b, pl.ds(kept, chunk), :]
            send_ref[b, h] = pgs[b, pl.ds(sent, chunk), :]

    if compact:
        @block_loop
        def _(b):
            ig_ref[b] = acc[rows_ref[b]].astype(ig_ref.dtype)
    else:
        ig_ref[...] = acc[...].astype(ig_ref.dtype)


def block_pass(features, hidden_grad, weights, row_ids, col_ids, row_count, low_bit, parts):
    tokens = features.shape[0]
    block_count, width, _ = weights.shape
    chunk = width // parts
    compact = block_count < row_count
    same = col_ids[:, None] == col_ids[None, :]
    first = jnp.argmax(same, axis=1).astype(jnp.int32)
    smem = pl.BlockSpec(memory_space=pltpu.SMEM)
    anyspace = pl.BlockSpec(memory_space=pl.ANY)
    vmem = pl.BlockSpec(memory_space=pltpu.VMEM)
    ig_rows = block_count if compact else row_count
    half = jax.ShapeDtypeStruct((block_count, parts // 2, chunk, width), jnp.float32)
    return pl.pallas_call(
        functools.partial(block_kernel, compact, chunk),
        out_shape=(
            jax.ShapeDtypeStruct((ig_rows, tokens, width), jnp.bfloat16),
            half,
            half,
        ),
        in_specs=[smem, smem, smem, smem, anyspace, anyspace, vmem],
        out_specs=(vmem, vmem, vmem),
        scratch_shapes=[
            pltpu.VMEM((block_count, tokens, width), jnp.bfloat16),
            pltpu.VMEM((block_count, tokens, width), jnp.bfloat16),
            pltpu.VMEM((block_count, tokens, width), jnp.float32),
            pltpu.VMEM((row_count, tokens, width), jnp.float32),
            pltpu.VMEM((block_count, width, width), jnp.float32),
            pltpu.SemaphoreType.DMA((2, block_count)),
        ],
        cost_estimate=pl.CostEstimate(
            flops=6 * block_count * tokens * width * width,
            transcendentals=block_count * tokens * width,
            bytes_accessed=block_count * width * (4 * tokens + 6 * width)
            + row_count * tokens * width * 2,
        ),
    )(row_ids, col_ids, first, low_bit, features, hidden_grad, weights)


def gather_over(x, axis):
    n = lax.axis_size(axis)
    return jnp.stack([x] + [shifted(x, axis, k) for k in range(1, n)])


def butterfly_gather(x, axis, bits):
    me = lax.axis_index(axis)
    held = x
    for bit in bits:
        other = swapped(held, axis, bit)
        mine_low = ((me >> bit) & 1) == 0
        held = jnp.where(mine_low, jnp.stack([held, other]), jnp.stack([other, held]))
    order = sorted(range(len(bits)), key=lambda a: -bits[len(bits) - 1 - a])
    perm = [order[i] for i in range(len(bits))] + list(range(len(bits), held.ndim))
    return jnp.transpose(held, perm)


def local(activations, out_grad, blocks, pattern, order):
    block_size = blocks.shape[-1]
    micro_count = activations.shape[1]
    tok_rows = activations.shape[1] * activations.shape[2]
    row_count = activations.shape[3] // block_size
    col_count = out_grad.shape[3] // block_size
    n_fsdp = lax.axis_size("fsdp")
    n_dp = lax.axis_size("dp")
    dp_bits = int(round(math.log2(n_dp)))
    assert 1 << dp_bits == n_dp and block_size % n_dp == 0
    chunk = block_size // n_dp
    me_dp = lax.axis_index("dp")

    own_blocks = blocks[0]
    blocks_dev = own_blocks.shape[0]

    assert n_fsdp % n_dp == 0
    per_dp = n_fsdp // n_dp
    weight_rows = blocks_dev * block_size
    assert 2 * blocks_dev <= block_size
    index_tile = jnp.zeros((16, block_size), jnp.bfloat16)
    index_tile = index_tile.at[0, : 2 * blocks_dev].set(
        pattern[0].reshape(-1).astype(jnp.bfloat16)
    )
    payload = jnp.concatenate([own_blocks.reshape(weight_rows, block_size), index_tile])
    fetched = []
    for m in range(per_dp):
        pairs = []
        for f in range(n_fsdp):
            for d in range(n_dp):
                k = d + n_dp * m
                pairs.append((((f - k) % n_fsdp) * n_dp + d, f * n_dp + d))
        fetched.append(lax.ppermute(payload, ("fsdp", "dp"), pairs))
    fetched = jnp.stack(fetched)
    pieces = butterfly_gather(fetched, "dp", list(reversed(range(dp_bits))))
    pieces = pieces.reshape((n_dp, per_dp) + payload.shape)
    pieces = jnp.transpose(pieces, (1, 0, 2, 3)).reshape((n_fsdp,) + payload.shape)
    weights = pieces[:, :weight_rows].reshape(n_fsdp * blocks_dev, block_size, block_size)
    all_indices = (
        pieces[:, weight_rows, : 2 * blocks_dev]
        .reshape(n_fsdp * blocks_dev, 2)
        .astype(jnp.int32)
    )

    row_ids = all_indices[:, 0]
    col_ids = all_indices[:, 1]
    low_bit = (me_dp & 1).astype(jnp.int32).reshape(1)
    input_grad, keep, send = block_pass(
        activations[0].reshape(tok_rows, -1),
        out_grad[0].reshape(tok_rows, -1),
        weights,
        row_ids,
        col_ids,
        row_count,
        low_bit,
        n_dp,
    )
    block_count = row_ids.shape[0]
    if block_count < row_count:
        payload = jnp.concatenate([input_grad.reshape(-1), row_ids.astype(jnp.bfloat16)])
        payload = passed_along(payload, "section", -1)
        got_rows = payload[input_grad.size :].astype(jnp.int32)
        got = payload[: input_grad.size].reshape(input_grad.shape)
        arrived = jnp.zeros((row_count,) + input_grad.shape[1:], jnp.bfloat16)
        arrived = arrived.at[got_rows].set(got)
    else:
        arrived = passed_along(input_grad, "section", -1)
    arrived = jnp.transpose(arrived, (1, 0, 2)).reshape(
        micro_count, activations.shape[2], activations.shape[3]
    )
    received = jnp.take(arrived, order, axis=0)

    held = keep + swapped(send, "dp", 0)
    held = held.reshape((n_fsdp, blocks_dev) + (2,) * (dp_bits - 1) + (chunk, block_size))
    for bit in range(1, dp_bits):
        axis_at = 2 + (dp_bits - 1 - bit)
        mine = (me_dp >> bit) & 1
        keep = lax.dynamic_index_in_dim(held, mine, axis_at, keepdims=False)
        send = lax.dynamic_index_in_dim(held, 1 - mine, axis_at, keepdims=False)
        held = keep + swapped(send.astype(jnp.bfloat16), "dp", bit).astype(jnp.float32)
    owned = held[0]
    for k in range(1, n_fsdp):
        owned = owned + shifted(held[k].astype(jnp.bfloat16), "fsdp", -k).astype(jnp.float32)
    relative = gather_over(owned, "dp")
    from_device = (me_dp - jnp.arange(n_dp, dtype=jnp.int32)) % n_dp
    full = jnp.take(relative, from_device, axis=0)
    full = jnp.transpose(full, (1, 0, 2, 3)).reshape(blocks_dev, block_size, block_size)
    grad_scale = jnp.sqrt(jnp.float32(tok_rows * n_fsdp * n_dp))
    return (received[None], (full / grad_scale)[None])


def solution(mesh):
    in_specs = (
        P("section", None, ("fsdp", "dp"), None),
        P("section", None, ("fsdp", "dp"), None),
        P("section", "fsdp", None, None),
        P("section", "fsdp", None),
        P(),
    )
    out_specs = (P("section", None, ("fsdp", "dp"), None), P("section", "fsdp", None, None))
    return jax.shard_map(local, mesh=mesh, in_specs=in_specs, out_specs=out_specs, check_vma=False)
```

```python
import functools
import math

import jax
import jax.numpy as jnp
from jax import lax
from jax.experimental import pallas as pl
from jax.experimental.pallas import tpu as pltpu
from jax.sharding import PartitionSpec as P


def passed_along(block, axis, distance):
    devices = range(lax.axis_size(axis))
    route = [(i - distance, i) for i in devices if i - distance in devices]
    return lax.ppermute(block, axis, route)


def shifted(x, axis, k):
    n = lax.axis_size(axis)
    return lax.ppermute(x, axis, [(i, (i + k) % n) for i in range(n)])


def swapped(x, axis, bit):
    n = lax.axis_size(axis)
    return lax.ppermute(x, axis, [(i, i ^ (1 << bit)) for i in range(n)])


def silu_slope(pre_act):
    sigmoid_val = jax.nn.sigmoid(pre_act)
    return sigmoid_val * (1.0 + pre_act * (1.0 - sigmoid_val))


def block_kernel(compact, chunk, rows_ref, cols_ref, bit_ref, feat_hbm, hid_hbm, pieces_ref,
                 ig_ref, keep_ref, send_ref, xs, hs, pr, acc, pgs, rep_ref, sems):
    width = pieces_ref.shape[-1]
    per_piece = (pieces_ref.shape[1] - 16) // width
    block_count = pieces_ref.shape[0] * per_piece

    def w_of(b):
        start = pl.multiple_of((b % per_piece) * width, width)
        return pieces_ref[b // per_piece, pl.ds(start, width), :]
    halves = keep_ref.shape[1]

    def block_loop(body):
        def step(b, carry):
            body(b)
            return carry

        lax.fori_loop(0, block_count, step, 0, unroll=min(block_count, 16))

    def copies(b):
        r = pl.multiple_of(rows_ref[b] * width, width)
        c = pl.multiple_of(cols_ref[b] * width, width)
        return (
            pltpu.make_async_copy(feat_hbm.at[:, pl.ds(r, width)], xs.at[b], sems.at[0, b]),
            pltpu.make_async_copy(hid_hbm.at[:, pl.ds(c, width)], hs.at[b], sems.at[1, b]),
        )

    @block_loop
    def _(b):
        for cp in copies(b):
            cp.start()

    for b in range(block_count):
        rep_ref[b] = b
    for b in range(block_count - 1, -1, -1):
        for a in range(b - 1, -1, -1):
            @pl.when(cols_ref[a] == cols_ref[b])
            def _():
                rep_ref[b] = a

    if compact:
        @block_loop
        def _(b):
            acc[rows_ref[b]] = jnp.zeros(acc.shape[1:], acc.dtype)
    else:
        acc[...] = jnp.zeros(acc.shape, acc.dtype)

    @block_loop
    def _(b):
        for cp in copies(b):
            cp.wait()
        pr[b] = jnp.dot(xs[b], w_of(b), preferred_element_type=jnp.float32)

    @block_loop
    def _(b):
        first = rep_ref[b]

        @pl.when(first != b)
        def _():
            pr[first] = pr[first] + pr[b]

    mine = bit_ref[0]

    @block_loop
    def _(b):
        pre_act = pr[rep_ref[b]]
        act = (hs[b].astype(jnp.float32) * silu_slope(pre_act)).astype(jnp.bfloat16)
        back = lax.dot_general(
            act, w_of(b), (((1,), (1,)), ((), ())), preferred_element_type=jnp.float32
        )
        row = rows_ref[b]
        acc[row] = acc[row] + back
        pgs[b] = lax.dot_general(
            xs[b], act, (((0,), (0,)), ((), ())), preferred_element_type=jnp.float32
        )
        for h in range(halves):
            kept = pl.multiple_of((2 * h + mine) * chunk, chunk)
            sent = pl.multiple_of((2 * h + 1 - mine) * chunk, chunk)
            keep_ref[b, h] = pgs[b, pl.ds(kept, chunk), :]
            send_ref[b, h] = pgs[b, pl.ds(sent, chunk), :]

    if compact:
        @block_loop
        def _(b):
            ig_ref[b] = acc[rows_ref[b]].astype(ig_ref.dtype)
    else:
        ig_ref[...] = acc[...].astype(ig_ref.dtype)


def block_pass(features, hidden_grad, pieces, row_ids, col_ids, row_count, low_bit, parts):
    tokens = features.shape[0]
    width = pieces.shape[-1]
    block_count = row_ids.shape[0]
    chunk = width // parts
    compact = block_count < row_count
    smem = pl.BlockSpec(memory_space=pltpu.SMEM)
    anyspace = pl.BlockSpec(memory_space=pl.ANY)
    vmem = pl.BlockSpec(memory_space=pltpu.VMEM)
    ig_rows = block_count if compact else row_count
    half = jax.ShapeDtypeStruct((block_count, parts // 2, chunk, width), jnp.float32)
    return pl.pallas_call(
        functools.partial(block_kernel, compact, chunk),
        out_shape=(
            jax.ShapeDtypeStruct((ig_rows, tokens, width), jnp.bfloat16),
            half,
            half,
        ),
        in_specs=[smem, smem, smem, anyspace, anyspace, vmem],
        out_specs=(vmem, vmem, vmem),
        scratch_shapes=[
            pltpu.VMEM((block_count, tokens, width), jnp.bfloat16),
            pltpu.VMEM((block_count, tokens, width), jnp.bfloat16),
            pltpu.VMEM((block_count, tokens, width), jnp.float32),
            pltpu.VMEM((row_count, tokens, width), jnp.float32),
            pltpu.VMEM((block_count, width, width), jnp.float32),
            pltpu.SMEM((block_count,), jnp.int32),
            pltpu.SemaphoreType.DMA((2, block_count)),
        ],
        cost_estimate=pl.CostEstimate(
            flops=6 * block_count * tokens * width * width,
            transcendentals=block_count * tokens * width,
            bytes_accessed=block_count * width * (4 * tokens + 6 * width)
            + row_count * tokens * width * 2,
        ),
    )(row_ids, col_ids, low_bit, features, hidden_grad, pieces)


def gather_over(x, axis):
    n = lax.axis_size(axis)
    return jnp.stack([x] + [shifted(x, axis, k) for k in range(1, n)])


def butterfly_gather(x, axis, bits):
    me = lax.axis_index(axis)
    held = x
    for bit in bits:
        other = swapped(held, axis, bit)
        mine_low = ((me >> bit) & 1) == 0
        held = jnp.where(mine_low, jnp.stack([held, other]), jnp.stack([other, held]))
    order = sorted(range(len(bits)), key=lambda a: -bits[len(bits) - 1 - a])
    perm = [order[i] for i in range(len(bits))] + list(range(len(bits), held.ndim))
    return jnp.transpose(held, perm)


def local(activations, out_grad, blocks, pattern, order):
    block_size = blocks.shape[-1]
    micro_count = activations.shape[1]
    tok_rows = activations.shape[1] * activations.shape[2]
    row_count = activations.shape[3] // block_size
    col_count = out_grad.shape[3] // block_size
    n_fsdp = lax.axis_size("fsdp")
    n_dp = lax.axis_size("dp")
    dp_bits = int(round(math.log2(n_dp)))
    assert 1 << dp_bits == n_dp and block_size % n_dp == 0
    chunk = block_size // n_dp
    me_dp = lax.axis_index("dp")

    own_blocks = blocks[0]
    blocks_dev = own_blocks.shape[0]

    assert n_fsdp % n_dp == 0
    per_dp = n_fsdp // n_dp
    weight_rows = blocks_dev * block_size
    assert 2 * blocks_dev <= block_size
    index_tile = jnp.zeros((16, block_size), jnp.bfloat16)
    index_tile = index_tile.at[0, : 2 * blocks_dev].set(
        pattern[0].reshape(-1).astype(jnp.bfloat16)
    )
    payload = jnp.concatenate([own_blocks.reshape(weight_rows, block_size), index_tile])
    fetched = []
    for m in range(per_dp):
        pairs = []
        for f in range(n_fsdp):
            for d in range(n_dp):
                k = d + n_dp * m
                pairs.append((((f - k) % n_fsdp) * n_dp + d, f * n_dp + d))
        fetched.append(lax.ppermute(payload, ("fsdp", "dp"), pairs))
    fetched = jnp.stack(fetched)
    pieces = butterfly_gather(fetched, "dp", list(reversed(range(dp_bits))))
    pieces = pieces.reshape((n_dp, per_dp) + payload.shape)
    pieces = jnp.transpose(pieces, (1, 0, 2, 3)).reshape((n_fsdp,) + payload.shape)
    all_indices = (
        pieces[:, weight_rows, : 2 * blocks_dev]
        .reshape(n_fsdp * blocks_dev, 2)
        .astype(jnp.int32)
    )

    row_ids = all_indices[:, 0]
    col_ids = all_indices[:, 1]
    low_bit = (me_dp & 1).astype(jnp.int32).reshape(1)
    input_grad, keep, send = block_pass(
        activations[0].reshape(tok_rows, -1),
        out_grad[0].reshape(tok_rows, -1),
        pieces,
        row_ids,
        col_ids,
        row_count,
        low_bit,
        n_dp,
    )
    block_count = row_ids.shape[0]
    if block_count < row_count:
        payload = jnp.concatenate([input_grad.reshape(-1), row_ids.astype(jnp.bfloat16)])
        payload = passed_along(payload, "section", -1)
        got_rows = payload[input_grad.size :].astype(jnp.int32)
        got = payload[: input_grad.size].reshape(input_grad.shape)
        arrived = jnp.zeros((row_count,) + input_grad.shape[1:], jnp.bfloat16)
        arrived = arrived.at[got_rows].set(got)
    else:
        arrived = passed_along(input_grad, "section", -1)
    arrived = jnp.transpose(arrived, (1, 0, 2)).reshape(
        micro_count, activations.shape[2], activations.shape[3]
    )
    received = jnp.take(arrived, order, axis=0)

    held = keep + swapped(send, "dp", 0)
    held = held.reshape((n_fsdp, blocks_dev) + (2,) * (dp_bits - 1) + (chunk, block_size))
    for bit in range(1, dp_bits):
        axis_at = 2 + (dp_bits - 1 - bit)
        mine = (me_dp >> bit) & 1
        keep = lax.dynamic_index_in_dim(held, mine, axis_at, keepdims=False)
        send = lax.dynamic_index_in_dim(held, 1 - mine, axis_at, keepdims=False)
        held = keep + swapped(send.astype(jnp.bfloat16), "dp", bit).astype(jnp.float32)
    owned = held[0]
    for k in range(1, n_fsdp):
        owned = owned + shifted(held[k].astype(jnp.bfloat16), "fsdp", -k).astype(jnp.float32)
    full = butterfly_gather(owned, "dp", list(reversed(range(dp_bits))))
    full = full.reshape((n_dp, blocks_dev, chunk, block_size))
    full = jnp.transpose(full, (1, 0, 2, 3)).reshape(blocks_dev, block_size, block_size)
    grad_scale = jnp.sqrt(jnp.float32(tok_rows * n_fsdp * n_dp))
    return (received[None], (full / grad_scale)[None])


def solution(mesh):
    in_specs = (
        P("section", None, ("fsdp", "dp"), None),
        P("section", None, ("fsdp", "dp"), None),
        P("section", "fsdp", None, None),
        P("section", "fsdp", None),
        P(),
    )
    out_specs = (P("section", None, ("fsdp", "dp"), None), P("section", "fsdp", None, None))
    return jax.shard_map(local, mesh=mesh, in_specs=in_specs, out_specs=out_specs, check_vma=False)
```

```python
import functools
import math

import jax
import jax.numpy as jnp
from jax import lax
from jax.experimental import pallas as pl
from jax.experimental.pallas import tpu as pltpu
from jax.sharding import PartitionSpec as P


def passed_along(block, axis, distance):
    devices = range(lax.axis_size(axis))
    route = [(i - distance, i) for i in devices if i - distance in devices]
    return lax.ppermute(block, axis, route)


def shifted(x, axis, k):
    n = lax.axis_size(axis)
    return lax.ppermute(x, axis, [(i, (i + k) % n) for i in range(n)])


def swapped(x, axis, bit):
    n = lax.axis_size(axis)
    return lax.ppermute(x, axis, [(i, i ^ (1 << bit)) for i in range(n)])


def silu_slope(pre_act):
    sigmoid_val = jax.nn.sigmoid(pre_act)
    return sigmoid_val * (1.0 + pre_act * (1.0 - sigmoid_val))


def block_kernel(compact, chunk, rows_ref, cols_ref, bit_ref, feat_hbm, hid_hbm, pieces_ref,
                 ig_ref, keep_ref, send_ref, xs, hs, pr, acc, pgs, rep_ref, sems):
    width = pieces_ref.shape[-1]
    per_piece = (pieces_ref.shape[1] - 16) // width
    block_count = pieces_ref.shape[0] * per_piece

    def w_of(b):
        start = pl.multiple_of((b % per_piece) * width, width)
        return pieces_ref[b // per_piece, pl.ds(start, width), :]
    halves = keep_ref.shape[1]

    def block_loop(body):
        def step(b, carry):
            body(b)
            return carry

        lax.fori_loop(0, block_count, step, 0, unroll=min(block_count, 16))

    def copies(b):
        r = pl.multiple_of(rows_ref[b] * width, width)
        c = pl.multiple_of(cols_ref[b] * width, width)
        return (
            pltpu.make_async_copy(feat_hbm.at[:, pl.ds(r, width)], xs.at[b], sems.at[0, b]),
            pltpu.make_async_copy(hid_hbm.at[:, pl.ds(c, width)], hs.at[b], sems.at[1, b]),
        )

    @block_loop
    def _(b):
        for cp in copies(b):
            cp.start()

    for b in range(block_count):
        rep_ref[b] = b
    for b in range(block_count - 1, -1, -1):
        for a in range(b - 1, -1, -1):
            @pl.when(cols_ref[a] == cols_ref[b])
            def _():
                rep_ref[b] = a

    if compact:
        @block_loop
        def _(b):
            acc[rows_ref[b]] = jnp.zeros(acc.shape[1:], acc.dtype)
    else:
        acc[...] = jnp.zeros(acc.shape, acc.dtype)

    @block_loop
    def _(b):
        for cp in copies(b):
            cp.wait()
        pr[b] = jnp.dot(xs[b], w_of(b), preferred_element_type=jnp.float32)

    @block_loop
    def _(b):
        first = rep_ref[b]

        @pl.when(first != b)
        def _():
            pr[first] = pr[first] + pr[b]

    mine = bit_ref[0]
    high = bit_ref[1]

    @block_loop
    def _(b):
        pre_act = pr[rep_ref[b]]
        act = (hs[b].astype(jnp.float32) * silu_slope(pre_act)).astype(jnp.bfloat16)
        back = lax.dot_general(
            act, w_of(b), (((1,), (1,)), ((), ())), preferred_element_type=jnp.float32
        )
        row = rows_ref[b]
        acc[row] = acc[row] + back
        pgs[b] = lax.dot_general(
            xs[b], act, (((0,), (0,)), ((), ())), preferred_element_type=jnp.float32
        )
        for h in range(halves):
            half = h ^ high
            kept = pl.multiple_of((2 * half + mine) * chunk, chunk)
            sent = pl.multiple_of((2 * half + 1 - mine) * chunk, chunk)
            keep_ref[b, h] = pgs[b, pl.ds(kept, chunk), :]
            send_ref[b, h] = pgs[b, pl.ds(sent, chunk), :]

    if compact:
        @block_loop
        def _(b):
            ig_ref[b] = acc[rows_ref[b]].astype(ig_ref.dtype)
    else:
        ig_ref[...] = acc[...].astype(ig_ref.dtype)


def block_pass(features, hidden_grad, pieces, row_ids, col_ids, row_count, low_bit, parts):
    tokens = features.shape[0]
    width = pieces.shape[-1]
    block_count = row_ids.shape[0]
    chunk = width // parts
    compact = block_count < row_count
    smem = pl.BlockSpec(memory_space=pltpu.SMEM)
    anyspace = pl.BlockSpec(memory_space=pl.ANY)
    vmem = pl.BlockSpec(memory_space=pltpu.VMEM)
    ig_rows = block_count if compact else row_count
    half = jax.ShapeDtypeStruct((block_count, parts // 2, chunk, width), jnp.float32)
    return pl.pallas_call(
        functools.partial(block_kernel, compact, chunk),
        out_shape=(
            jax.ShapeDtypeStruct((ig_rows, tokens, width), jnp.bfloat16),
            half,
            half,
        ),
        in_specs=[smem, smem, smem, anyspace, anyspace, vmem],
        out_specs=(vmem, vmem, vmem),
        scratch_shapes=[
            pltpu.VMEM((block_count, tokens, width), jnp.bfloat16),
            pltpu.VMEM((block_count, tokens, width), jnp.bfloat16),
            pltpu.VMEM((block_count, tokens, width), jnp.float32),
            pltpu.VMEM((row_count, tokens, width), jnp.float32),
            pltpu.VMEM((block_count, width, width), jnp.float32),
            pltpu.SMEM((block_count,), jnp.int32),
            pltpu.SemaphoreType.DMA((2, block_count)),
        ],
        cost_estimate=pl.CostEstimate(
            flops=6 * block_count * tokens * width * width,
            transcendentals=block_count * tokens * width,
            bytes_accessed=block_count * width * (4 * tokens + 6 * width)
            + row_count * tokens * width * 2,
        ),
    )(row_ids, col_ids, low_bit, features, hidden_grad, pieces)


def gather_over(x, axis):
    n = lax.axis_size(axis)
    return jnp.stack([x] + [shifted(x, axis, k) for k in range(1, n)])


def butterfly_gather(x, axis, bits):
    me = lax.axis_index(axis)
    held = x
    for bit in bits:
        other = swapped(held, axis, bit)
        mine_low = ((me >> bit) & 1) == 0
        held = jnp.where(mine_low, jnp.stack([held, other]), jnp.stack([other, held]))
    order = sorted(range(len(bits)), key=lambda a: -bits[len(bits) - 1 - a])
    perm = [order[i] for i in range(len(bits))] + list(range(len(bits), held.ndim))
    return jnp.transpose(held, perm)


def local(activations, out_grad, blocks, pattern, order):
    block_size = blocks.shape[-1]
    micro_count = activations.shape[1]
    tok_rows = activations.shape[1] * activations.shape[2]
    row_count = activations.shape[3] // block_size
    col_count = out_grad.shape[3] // block_size
    n_fsdp = lax.axis_size("fsdp")
    n_dp = lax.axis_size("dp")
    dp_bits = int(round(math.log2(n_dp)))
    assert 1 << dp_bits == n_dp and block_size % n_dp == 0
    chunk = block_size // n_dp
    me_dp = lax.axis_index("dp")

    own_blocks = blocks[0]
    blocks_dev = own_blocks.shape[0]

    assert n_fsdp % n_dp == 0
    per_dp = n_fsdp // n_dp
    weight_rows = blocks_dev * block_size
    assert 2 * blocks_dev <= block_size
    index_tile = jnp.zeros((16, block_size), jnp.bfloat16)
    index_tile = index_tile.at[0, : 2 * blocks_dev].set(
        pattern[0].reshape(-1).astype(jnp.bfloat16)
    )
    payload = jnp.concatenate([own_blocks.reshape(weight_rows, block_size), index_tile])
    fetched = []
    for m in range(per_dp):
        pairs = []
        for f in range(n_fsdp):
            for d in range(n_dp):
                k = d + n_dp * m
                pairs.append((((f - k) % n_fsdp) * n_dp + d, f * n_dp + d))
        fetched.append(lax.ppermute(payload, ("fsdp", "dp"), pairs))
    fetched = jnp.stack(fetched)
    pieces = butterfly_gather(fetched, "dp", list(reversed(range(dp_bits))))
    pieces = pieces.reshape((n_dp, per_dp) + payload.shape)
    pieces = jnp.transpose(pieces, (1, 0, 2, 3)).reshape((n_fsdp,) + payload.shape)
    all_indices = (
        pieces[:, weight_rows, : 2 * blocks_dev]
        .reshape(n_fsdp * blocks_dev, 2)
        .astype(jnp.int32)
    )

    row_ids = all_indices[:, 0]
    col_ids = all_indices[:, 1]
    assert n_dp == 4
    low_bit = jnp.stack([me_dp & 1, (me_dp >> 1) & 1]).astype(jnp.int32)
    input_grad, keep, send = block_pass(
        activations[0].reshape(tok_rows, -1),
        out_grad[0].reshape(tok_rows, -1),
        pieces,
        row_ids,
        col_ids,
        row_count,
        low_bit,
        n_dp,
    )
    block_count = row_ids.shape[0]
    if block_count < row_count:
        payload = jnp.concatenate([input_grad.reshape(-1), row_ids.astype(jnp.bfloat16)])
        payload = passed_along(payload, "section", -1)
        got_rows = payload[input_grad.size :].astype(jnp.int32)
        got = payload[: input_grad.size].reshape(input_grad.shape)
        arrived = jnp.zeros((row_count,) + input_grad.shape[1:], jnp.bfloat16)
        arrived = arrived.at[got_rows].set(got)
    else:
        arrived = passed_along(input_grad, "section", -1)
    arrived = jnp.transpose(arrived, (1, 0, 2)).reshape(
        micro_count, activations.shape[2], activations.shape[3]
    )
    received = jnp.take(arrived, order, axis=0)

    held = keep + swapped(send, "dp", 0)
    held = held.reshape((n_fsdp, blocks_dev, 2, chunk, block_size))
    held = held[:, :, 0] + swapped(held[:, :, 1].astype(jnp.bfloat16), "dp", 1).astype(
        jnp.float32
    )
    owned = held[0]
    for k in range(1, n_fsdp):
        owned = owned + shifted(held[k].astype(jnp.bfloat16), "fsdp", -k).astype(jnp.float32)
    full = butterfly_gather(owned, "dp", list(reversed(range(dp_bits))))
    full = full.reshape((n_dp, blocks_dev, chunk, block_size))
    full = jnp.transpose(full, (1, 0, 2, 3)).reshape(blocks_dev, block_size, block_size)
    grad_scale = jnp.sqrt(jnp.float32(tok_rows * n_fsdp * n_dp))
    return (received[None], (full / grad_scale)[None])


def solution(mesh):
    in_specs = (
        P("section", None, ("fsdp", "dp"), None),
        P("section", None, ("fsdp", "dp"), None),
        P("section", "fsdp", None, None),
        P("section", "fsdp", None),
        P(),
    )
    out_specs = (P("section", None, ("fsdp", "dp"), None), P("section", "fsdp", None, None))
    return jax.shard_map(local, mesh=mesh, in_specs=in_specs, out_specs=out_specs, check_vma=False)
```

```python
import functools
import math

import jax
import jax.numpy as jnp
from jax import lax
from jax.experimental import pallas as pl
from jax.experimental.pallas import tpu as pltpu
from jax.sharding import PartitionSpec as P


def passed_along(block, axis, distance):
    devices = range(lax.axis_size(axis))
    route = [(i - distance, i) for i in devices if i - distance in devices]
    return lax.ppermute(block, axis, route)


def shifted(x, axis, k):
    n = lax.axis_size(axis)
    return lax.ppermute(x, axis, [(i, (i + k) % n) for i in range(n)])


def swapped(x, axis, bit):
    n = lax.axis_size(axis)
    return lax.ppermute(x, axis, [(i, i ^ (1 << bit)) for i in range(n)])


def silu_slope(pre_act):
    sigmoid_val = jax.nn.sigmoid(pre_act)
    return sigmoid_val * (1.0 + pre_act * (1.0 - sigmoid_val))


def block_kernel(compact, chunk, rows_ref, cols_ref, bit_ref, feat_hbm, hid_hbm, pieces_ref,
                 ig_ref, keep_ref, send_ref, xs, hs, pr, acc, pgs, rep_ref, sems):
    width = pieces_ref.shape[-1]
    per_piece = (pieces_ref.shape[1] - 16) // width
    block_count = pieces_ref.shape[0] * per_piece

    def w_of(b):
        start = pl.multiple_of((b % per_piece) * width, width)
        return pieces_ref[b // per_piece, pl.ds(start, width), :]
    halves = keep_ref.shape[1]

    def block_loop(body):
        def step(b, carry):
            body(b)
            return carry

        lax.fori_loop(0, block_count, step, 0, unroll=min(block_count, 16))

    def copies(b):
        r = pl.multiple_of(rows_ref[b] * width, width)
        c = pl.multiple_of(cols_ref[b] * width, width)
        return (
            pltpu.make_async_copy(feat_hbm.at[:, pl.ds(r, width)], xs.at[b], sems.at[0, b]),
            pltpu.make_async_copy(hid_hbm.at[:, pl.ds(c, width)], hs.at[b], sems.at[1, b]),
        )

    @block_loop
    def _(b):
        for cp in copies(b):
            cp.start()

    for b in range(block_count):
        rep_ref[b] = b
    for b in range(block_count - 1, -1, -1):
        for a in range(b - 1, -1, -1):
            @pl.when(cols_ref[a] == cols_ref[b])
            def _():
                rep_ref[b] = a

    if compact:
        @block_loop
        def _(b):
            acc[rows_ref[b]] = jnp.zeros(acc.shape[1:], acc.dtype)
    else:
        acc[...] = jnp.zeros(acc.shape, acc.dtype)

    @block_loop
    def _(b):
        for cp in copies(b):
            cp.wait()
        pr[b] = jnp.dot(xs[b], w_of(b), preferred_element_type=jnp.float32)

    @block_loop
    def _(b):
        first = rep_ref[b]

        @pl.when(first != b)
        def _():
            pr[first] = pr[first] + pr[b]

    mine = bit_ref[0]

    @block_loop
    def _(b):
        pre_act = pr[rep_ref[b]]
        act = (hs[b].astype(jnp.float32) * silu_slope(pre_act)).astype(jnp.bfloat16)
        back = lax.dot_general(
            act, w_of(b), (((1,), (1,)), ((), ())), preferred_element_type=jnp.float32
        )
        row = rows_ref[b]
        acc[row] = acc[row] + back
        pgs[b] = lax.dot_general(
            xs[b], act, (((0,), (0,)), ((), ())), preferred_element_type=jnp.float32
        )
        for h in range(halves):
            kept = pl.multiple_of((2 * h + mine) * chunk, chunk)
            sent = pl.multiple_of((2 * h + 1 - mine) * chunk, chunk)
            keep_ref[b, h] = pgs[b, pl.ds(kept, chunk), :]
            send_ref[b, h] = pgs[b, pl.ds(sent, chunk), :]

    if compact:
        @block_loop
        def _(b):
            ig_ref[b] = acc[rows_ref[b]].astype(ig_ref.dtype)
    else:
        ig_ref[...] = acc[...].astype(ig_ref.dtype)


def block_pass(features, hidden_grad, pieces, row_ids, col_ids, row_count, low_bit, parts):
    tokens = features.shape[0]
    width = pieces.shape[-1]
    block_count = row_ids.shape[0]
    chunk = width // parts
    compact = block_count < row_count
    smem = pl.BlockSpec(memory_space=pltpu.SMEM)
    anyspace = pl.BlockSpec(memory_space=pl.ANY)
    vmem = pl.BlockSpec(memory_space=pltpu.VMEM)
    ig_rows = block_count if compact else row_count
    half = jax.ShapeDtypeStruct((block_count, parts // 2, chunk, width), jnp.float32)
    return pl.pallas_call(
        functools.partial(block_kernel, compact, chunk),
        out_shape=(
            jax.ShapeDtypeStruct((ig_rows, tokens, width), jnp.bfloat16),
            half,
            half,
        ),
        in_specs=[smem, smem, smem, anyspace, anyspace, vmem],
        out_specs=(vmem, vmem, vmem),
        scratch_shapes=[
            pltpu.VMEM((block_count, tokens, width), jnp.bfloat16),
            pltpu.VMEM((block_count, tokens, width), jnp.bfloat16),
            pltpu.VMEM((block_count, tokens, width), jnp.float32),
            pltpu.VMEM((row_count, tokens, width), jnp.float32),
            pltpu.VMEM((block_count, width, width), jnp.float32),
            pltpu.SMEM((block_count,), jnp.int32),
            pltpu.SemaphoreType.DMA((2, block_count)),
        ],
        cost_estimate=pl.CostEstimate(
            flops=6 * block_count * tokens * width * width,
            transcendentals=block_count * tokens * width,
            bytes_accessed=block_count * width * (4 * tokens + 6 * width)
            + row_count * tokens * width * 2,
        ),
    )(row_ids, col_ids, low_bit, features, hidden_grad, pieces)


def gather_over(x, axis):
    n = lax.axis_size(axis)
    return jnp.stack([x] + [shifted(x, axis, k) for k in range(1, n)])


def butterfly_gather(x, axis, bits):
    me = lax.axis_index(axis)
    held = x
    for bit in bits:
        other = swapped(held, axis, bit)
        mine_low = ((me >> bit) & 1) == 0
        held = jnp.where(mine_low, jnp.stack([held, other]), jnp.stack([other, held]))
    order = sorted(range(len(bits)), key=lambda a: -bits[len(bits) - 1 - a])
    perm = [order[i] for i in range(len(bits))] + list(range(len(bits), held.ndim))
    return jnp.transpose(held, perm)


def local(activations, out_grad, blocks, pattern, order):
    block_size = blocks.shape[-1]
    micro_count = activations.shape[1]
    tok_rows = activations.shape[1] * activations.shape[2]
    row_count = activations.shape[3] // block_size
    col_count = out_grad.shape[3] // block_size
    n_fsdp = lax.axis_size("fsdp")
    n_dp = lax.axis_size("dp")
    dp_bits = int(round(math.log2(n_dp)))
    assert 1 << dp_bits == n_dp and block_size % n_dp == 0
    chunk = block_size // n_dp
    me_dp = lax.axis_index("dp")

    own_blocks = blocks[0]
    blocks_dev = own_blocks.shape[0]

    assert n_fsdp % n_dp == 0
    per_dp = n_fsdp // n_dp
    weight_rows = blocks_dev * block_size
    assert 2 * blocks_dev <= block_size
    index_tile = jnp.zeros((16, block_size), jnp.bfloat16)
    index_tile = index_tile.at[0, : 2 * blocks_dev].set(
        pattern[0].reshape(-1).astype(jnp.bfloat16)
    )
    payload = jnp.concatenate([own_blocks.reshape(weight_rows, block_size), index_tile])
    fetched = []
    for m in range(per_dp):
        pairs = []
        for f in range(n_fsdp):
            for d in range(n_dp):
                k = d + n_dp * m
                pairs.append((((f - k) % n_fsdp) * n_dp + d, f * n_dp + d))
        fetched.append(lax.ppermute(payload, ("fsdp", "dp"), pairs))
    fetched = jnp.stack(fetched)
    pieces = butterfly_gather(fetched, "dp", list(reversed(range(dp_bits))))
    pieces = pieces.reshape((n_dp, per_dp) + payload.shape)
    pieces = jnp.transpose(pieces, (1, 0, 2, 3)).reshape((n_fsdp,) + payload.shape)
    all_indices = (
        pieces[:, weight_rows, : 2 * blocks_dev]
        .reshape(n_fsdp * blocks_dev, 2)
        .astype(jnp.int32)
    )

    row_ids = all_indices[:, 0]
    col_ids = all_indices[:, 1]
    low_bit = (me_dp & 1).astype(jnp.int32).reshape(1)
    input_grad, keep, send = block_pass(
        activations[0].reshape(tok_rows, -1),
        out_grad[0].reshape(tok_rows, -1),
        pieces,
        row_ids,
        col_ids,
        row_count,
        low_bit,
        n_dp,
    )
    block_count = row_ids.shape[0]
    if block_count < row_count:
        payload = jnp.concatenate([input_grad.reshape(-1), row_ids.astype(jnp.bfloat16)])
        payload = passed_along(payload, "section", -1)
        got_rows = payload[input_grad.size :].astype(jnp.int32)
        got = payload[: input_grad.size].reshape(input_grad.shape)
        arrived = jnp.zeros((row_count,) + input_grad.shape[1:], jnp.bfloat16)
        arrived = arrived.at[got_rows].set(got)
    else:
        arrived = passed_along(input_grad, "section", -1)
    arrived = jnp.transpose(arrived, (1, 0, 2)).reshape(
        micro_count, activations.shape[2], activations.shape[3]
    )
    received = jnp.take(arrived, order, axis=0)

    held = keep + swapped(send, "dp", 0)
    held = held.reshape((n_fsdp, blocks_dev) + (2,) * (dp_bits - 1) + (chunk, block_size))
    for bit in range(1, dp_bits):
        axis_at = 2 + (dp_bits - 1 - bit)
        mine = (me_dp >> bit) & 1
        keep = lax.dynamic_index_in_dim(held, mine, axis_at, keepdims=False)
        send = lax.dynamic_index_in_dim(held, 1 - mine, axis_at, keepdims=False)
        held = keep + swapped(send.astype(jnp.bfloat16), "dp", bit).astype(jnp.float32)
    owned = held[0]
    for k in range(1, n_fsdp):
        owned = owned + shifted(held[k].astype(jnp.bfloat16), "fsdp", -k).astype(jnp.float32)
    grad_scale = jnp.sqrt(jnp.float32(tok_rows * n_fsdp * n_dp))
    full = butterfly_gather(owned / grad_scale, "dp", list(reversed(range(dp_bits))))
    full = full.reshape((n_dp, blocks_dev, chunk, block_size))
    full = jnp.transpose(full, (1, 0, 2, 3)).reshape(blocks_dev, block_size, block_size)
    return (received[None], full[None])


def solution(mesh):
    in_specs = (
        P("section", None, ("fsdp", "dp"), None),
        P("section", None, ("fsdp", "dp"), None),
        P("section", "fsdp", None, None),
        P("section", "fsdp", None),
        P(),
    )
    out_specs = (P("section", None, ("fsdp", "dp"), None), P("section", "fsdp", None, None))
    return jax.shard_map(local, mesh=mesh, in_specs=in_specs, out_specs=out_specs, check_vma=False)
```

```python
import functools
import math

import jax
import jax.numpy as jnp
from jax import lax
from jax.experimental import pallas as pl
from jax.experimental.pallas import tpu as pltpu
from jax.sharding import PartitionSpec as P


def passed_along(block, axis, distance):
    devices = range(lax.axis_size(axis))
    route = [(i - distance, i) for i in devices if i - distance in devices]
    return lax.ppermute(block, axis, route)


def shifted(x, axis, k):
    n = lax.axis_size(axis)
    return lax.ppermute(x, axis, [(i, (i + k) % n) for i in range(n)])


def swapped(x, axis, bit):
    n = lax.axis_size(axis)
    return lax.ppermute(x, axis, [(i, i ^ (1 << bit)) for i in range(n)])


def silu_slope(pre_act):
    sigmoid_val = jax.nn.sigmoid(pre_act)
    return sigmoid_val * (1.0 + pre_act * (1.0 - sigmoid_val))


def block_kernel(compact, chunk, rows_ref, cols_ref, bit_ref, feat_hbm, hid_hbm, pieces_ref,
                 ig_ref, keep_ref, send_ref, xs, hs, pr, acc, pgs, rep_ref, sems):
    width = pieces_ref.shape[-1]
    per_piece = (pieces_ref.shape[1] - 16) // width
    block_count = pieces_ref.shape[0] * per_piece

    def w_of(b):
        start = pl.multiple_of((b % per_piece) * width, width)
        return pieces_ref[b // per_piece, pl.ds(start, width), :]
    halves = keep_ref.shape[1]

    def block_loop(body):
        def step(b, carry):
            body(b)
            return carry

        lax.fori_loop(0, block_count, step, 0, unroll=min(block_count, 16))

    def copies(b):
        r = pl.multiple_of(rows_ref[b] * width, width)
        c = pl.multiple_of(cols_ref[b] * width, width)
        return (
            pltpu.make_async_copy(feat_hbm.at[:, pl.ds(r, width)], xs.at[b], sems.at[0, b]),
            pltpu.make_async_copy(hid_hbm.at[:, pl.ds(c, width)], hs.at[b], sems.at[1, b]),
        )

    @block_loop
    def _(b):
        for cp in copies(b):
            cp.start()

    for b in range(block_count):
        rep_ref[b] = b
    for b in range(block_count - 1, -1, -1):
        for a in range(b - 1, -1, -1):
            @pl.when(cols_ref[a] == cols_ref[b])
            def _():
                rep_ref[b] = a

    if compact:
        @block_loop
        def _(b):
            acc[rows_ref[b]] = jnp.zeros(acc.shape[1:], acc.dtype)
    else:
        acc[...] = jnp.zeros(acc.shape, acc.dtype)

    @block_loop
    def _(b):
        for cp in copies(b):
            cp.wait()
        pr[b] = jnp.dot(xs[b], w_of(b), preferred_element_type=jnp.float32)

    @block_loop
    def _(b):
        first = rep_ref[b]

        @pl.when(first != b)
        def _():
            pr[first] = pr[first] + pr[b]

    mine = bit_ref[0]

    @block_loop
    def _(b):
        pre_act = pr[rep_ref[b]]
        act = (hs[b].astype(jnp.float32) * silu_slope(pre_act)).astype(jnp.bfloat16)
        back = lax.dot_general(
            act, w_of(b), (((1,), (1,)), ((), ())), preferred_element_type=jnp.float32
        )
        row = rows_ref[b]
        acc[row] = acc[row] + back
        pgs[b] = lax.dot_general(
            xs[b], act, (((0,), (0,)), ((), ())), preferred_element_type=jnp.float32
        )
        for h in range(halves):
            kept = pl.multiple_of((2 * h + mine) * chunk, chunk)
            sent = pl.multiple_of((2 * h + 1 - mine) * chunk, chunk)
            keep_ref[b, h] = pgs[b, pl.ds(kept, chunk), :]
            send_ref[b, h] = pgs[b, pl.ds(sent, chunk), :]

    if compact:
        @block_loop
        def _(b):
            ig_ref[b] = acc[rows_ref[b]].astype(ig_ref.dtype)
    else:
        ig_ref[...] = acc[...].astype(ig_ref.dtype)


def block_pass(features, hidden_grad, pieces, row_ids, col_ids, row_count, low_bit, parts):
    tokens = features.shape[0]
    width = pieces.shape[-1]
    block_count = row_ids.shape[0]
    chunk = width // parts
    compact = block_count < row_count
    smem = pl.BlockSpec(memory_space=pltpu.SMEM)
    anyspace = pl.BlockSpec(memory_space=pl.ANY)
    vmem = pl.BlockSpec(memory_space=pltpu.VMEM)
    ig_rows = block_count if compact else row_count
    half = jax.ShapeDtypeStruct((block_count, parts // 2, chunk, width), jnp.float32)
    return pl.pallas_call(
        functools.partial(block_kernel, compact, chunk),
        out_shape=(
            jax.ShapeDtypeStruct((ig_rows, tokens, width), jnp.bfloat16),
            half,
            half,
        ),
        in_specs=[smem, smem, smem, anyspace, anyspace, vmem],
        out_specs=(vmem, vmem, vmem),
        scratch_shapes=[
            pltpu.VMEM((block_count, tokens, width), jnp.bfloat16),
            pltpu.VMEM((block_count, tokens, width), jnp.bfloat16),
            pltpu.VMEM((block_count, tokens, width), jnp.float32),
            pltpu.VMEM((row_count, tokens, width), jnp.float32),
            pltpu.VMEM((block_count, width, width), jnp.float32),
            pltpu.SMEM((block_count,), jnp.int32),
            pltpu.SemaphoreType.DMA((2, block_count)),
        ],
        cost_estimate=pl.CostEstimate(
            flops=6 * block_count * tokens * width * width,
            transcendentals=block_count * tokens * width,
            bytes_accessed=block_count * width * (4 * tokens + 6 * width)
            + row_count * tokens * width * 2,
        ),
    )(row_ids, col_ids, low_bit, features, hidden_grad, pieces)


def gather_over(x, axis):
    n = lax.axis_size(axis)
    return jnp.stack([x] + [shifted(x, axis, k) for k in range(1, n)])


def butterfly_gather(x, axis, bits):
    me = lax.axis_index(axis)
    held = x
    for bit in bits:
        other = swapped(held, axis, bit)
        mine_low = ((me >> bit) & 1) == 0
        held = jnp.where(mine_low, jnp.stack([held, other]), jnp.stack([other, held]))
    order = sorted(range(len(bits)), key=lambda a: -bits[len(bits) - 1 - a])
    perm = [order[i] for i in range(len(bits))] + list(range(len(bits), held.ndim))
    return jnp.transpose(held, perm)


def local(activations, out_grad, blocks, pattern, order):
    block_size = blocks.shape[-1]
    micro_count = activations.shape[1]
    tok_rows = activations.shape[1] * activations.shape[2]
    row_count = activations.shape[3] // block_size
    col_count = out_grad.shape[3] // block_size
    n_fsdp = lax.axis_size("fsdp")
    n_dp = lax.axis_size("dp")
    dp_bits = int(round(math.log2(n_dp)))
    assert 1 << dp_bits == n_dp and block_size % n_dp == 0
    chunk = block_size // n_dp
    me_dp = lax.axis_index("dp")

    own_blocks = blocks[0]
    blocks_dev = own_blocks.shape[0]

    assert n_fsdp % n_dp == 0
    per_dp = n_fsdp // n_dp
    weight_rows = blocks_dev * block_size
    assert 2 * blocks_dev <= block_size
    index_tile = jnp.zeros((16, block_size), jnp.bfloat16)
    index_tile = index_tile.at[0, : 2 * blocks_dev].set(
        pattern[0].reshape(-1).astype(jnp.bfloat16)
    )
    payload = jnp.concatenate([own_blocks.reshape(weight_rows, block_size), index_tile])
    fetched = []
    for m in range(per_dp):
        pairs = []
        for f in range(n_fsdp):
            for d in range(n_dp):
                k = d + n_dp * m
                pairs.append((((f - k) % n_fsdp) * n_dp + d, f * n_dp + d))
        fetched.append(lax.ppermute(payload, ("fsdp", "dp"), pairs))
    fetched = jnp.stack(fetched)
    pieces = butterfly_gather(fetched, "dp", list(reversed(range(dp_bits))))
    pieces = pieces.reshape((n_dp, per_dp) + payload.shape)
    pieces = jnp.transpose(pieces, (1, 0, 2, 3)).reshape((n_fsdp,) + payload.shape)
    all_indices = (
        pieces[:, weight_rows, : 2 * blocks_dev]
        .reshape(n_fsdp * blocks_dev, 2)
        .astype(jnp.int32)
    )

    row_ids = all_indices[:, 0]
    col_ids = all_indices[:, 1]
    low_bit = (me_dp & 1).astype(jnp.int32).reshape(1)
    input_grad, keep, send = block_pass(
        activations[0].reshape(tok_rows, -1),
        out_grad[0].reshape(tok_rows, -1),
        pieces,
        row_ids,
        col_ids,
        row_count,
        low_bit,
        n_dp,
    )
    block_count = row_ids.shape[0]
    if block_count < row_count:
        payload = jnp.concatenate([input_grad.reshape(-1), row_ids.astype(jnp.bfloat16)])
        payload = passed_along(payload, "section", -1)
        got_rows = payload[input_grad.size :].astype(jnp.int32)
        got = payload[: input_grad.size].reshape(input_grad.shape)
        arrived = jnp.zeros((row_count,) + input_grad.shape[1:], jnp.bfloat16)
        arrived = arrived.at[got_rows].set(got)
    else:
        arrived = passed_along(input_grad, "section", -1)
    arrived = jnp.transpose(arrived, (1, 0, 2)).reshape(
        micro_count, activations.shape[2], activations.shape[3]
    )
    received = jnp.take(arrived, order, axis=0)

    held = keep + swapped(send, "dp", 0)
    held = held.reshape((n_fsdp, blocks_dev) + (2,) * (dp_bits - 1) + (chunk, block_size))
    for bit in range(1, dp_bits):
        axis_at = 2 + (dp_bits - 1 - bit)
        mine = (me_dp >> bit) & 1
        keep = lax.dynamic_index_in_dim(held, mine, axis_at, keepdims=False)
        send = lax.dynamic_index_in_dim(held, 1 - mine, axis_at, keepdims=False)
        held = keep + swapped(send.astype(jnp.bfloat16), "dp", bit).astype(jnp.float32)
    owned = held[0]
    for k in range(1, n_fsdp):
        owned = owned + shifted(held[k].astype(jnp.bfloat16), "fsdp", -k).astype(jnp.float32)
    full = owned
    for level, bit in enumerate(reversed(range(dp_bits))):
        other = swapped(full, "dp", bit)
        mine_low = ((me_dp >> bit) & 1) == 0
        at = 1 + level
        full = jnp.where(
            mine_low, jnp.stack([full, other], axis=at), jnp.stack([other, full], axis=at)
        )
    full = full.reshape(blocks_dev, block_size, block_size)
    grad_scale = jnp.sqrt(jnp.float32(tok_rows * n_fsdp * n_dp))
    return (received[None], (full / grad_scale)[None])


def solution(mesh):
    in_specs = (
        P("section", None, ("fsdp", "dp"), None),
        P("section", None, ("fsdp", "dp"), None),
        P("section", "fsdp", None, None),
        P("section", "fsdp", None),
        P(),
    )
    out_specs = (P("section", None, ("fsdp", "dp"), None), P("section", "fsdp", None, None))
    return jax.shard_map(local, mesh=mesh, in_specs=in_specs, out_specs=out_specs, check_vma=False)
```
